256 devices in a mesh: seq: 64 (over y, z, core), head: 4 (over x).
Axes of the slice: x: 4, y: 4, z: 8, core: 2. Of those that a mesh axis runs over, the one named last changes fastest.
Arguments:
- queries: bfloat16 [8192, 1024], P('seq', 'head'), may hold values from -6 to 6
- raw_keys: bfloat16 [8192, 1024], P('seq', 'head'), may hold values from -6 to 6
- values: bfloat16 [8192, 1024], P('seq', 'head'), may hold values from -6 to 6
- write_rate: float32 [8192, 8], P('seq', 'head'), may hold values from 0.0005 to 1
- out_weight: bfloat16 [1024, 1024], P('head'), may hold values from -0.1875 to 0.1875
- out_grad: bfloat16 [8192, 1024], P('seq', 'head'), may hold values from -6 to 6
Outputs:
- layer_out: bfloat16 [8192, 1024], P('seq', 'head')
- query_grad: bfloat16 [8192, 1024], P('seq', 'head')
- key_grad: bfloat16 [8192, 1024], P('seq', 'head')
- value_grad: bfloat16 [8192, 1024], P('seq', 'head')
- rate_grad: float32 [8192, 8], P('seq', 'head')
The draws below stay inside these ranges and needn't reach their ends.
All inputs are finite; a program needn't handle non-finite values.
Results may differ from the reference program's by a relative error of at most 0.0049.
Values may be sent and summed in bfloat16 or wider, within the bound.
No kernel may reach another device: no remote copies, remote signals or barrier semaphores. Data moves between devices by JAX's collectives and lax.ppermute only.
A program may use at most 128 MiB of HBM per device.

```python
import math
import jax
import jax.numpy as jnp
from jax import lax

D = 1024
HEAD_TOTAL = 8
DH = 128
BLOCK = 64
TOKEN_TOTAL = 8192


def draw_write_rate(key, part):
    level_random_key, coarse_random_key, initial_random_key, spike_random_key = jax.random.split(key, 4)
    lowest = 0.001
    highest_level = 0.3
    noise_level = jnp.exp(jax.random.uniform(level_random_key, (HEAD_TOTAL,), jnp.float32, math.log(lowest), math.log(highest_level)))
    coarse_input = jax.random.uniform(coarse_random_key, (TOKEN_TOTAL, HEAD_TOTAL), jnp.float32, 0.5, 2.0)
    starts = jax.random.randint(initial_random_key, (4, 1), 0, TOKEN_TOTAL)
    position = jnp.arange(TOKEN_TOTAL, dtype=jnp.int32)[None, :]
    inner_result = jnp.any(jnp.abs(position - starts) < 32, axis=0)
    spike_input = jax.random.uniform(spike_random_key, (TOKEN_TOTAL, HEAD_TOTAL), jnp.float32, 0.4, 1.0)
    decay_rate = jnp.where(inner_result[:, None], spike_input, noise_level[None, :] * coarse_input)
    return jnp.clip(decay_rate, 0.0005, 1.0)


def levels(own_key, shape, cuts, least, top_value):
    level = 1.0
    for axis_at, blocks in cuts:
        steps = jax.random.uniform(jax.random.fold_in(jax.random.fold_in(own_key, 6), axis_at), (blocks,), jnp.float32, least / len(cuts), top_value / len(cuts))
        level = level * jnp.repeat(jnp.exp(steps), shape[axis_at] // blocks).reshape((-1,) + (1,) * (len(shape) - 1 - axis_at))
    return level


def scatter_about(own_key, shape, scale, most, cuts=(), held_as=jnp.bfloat16):
    drawn = scale * jax.random.normal(own_key, shape, jnp.float32)
    if cuts:
        drawn = drawn * levels(own_key, shape, cuts, -0.22, 0.18)
    return jnp.clip(drawn, -most, most).astype(held_as)


def setup_inputs(seed: int = 0) -> dict:
    key_of = jax.random.split(jax.random.key(seed), 7)
    queries = scatter_about(key_of[0], (TOKEN_TOTAL, HEAD_TOTAL * DH), 1.0, 6.0, ((0, 64), (1, 4)))
    raw_keys = scatter_about(key_of[1], (TOKEN_TOTAL, HEAD_TOTAL * DH), 1.0, 6.0, ((0, 64), (1, 4)))
    values = scatter_about(key_of[2], (TOKEN_TOTAL, HEAD_TOTAL * DH), 1.0, 6.0, ((0, 64), (1, 4)))
    write_rate = draw_write_rate(jax.random.fold_in(key_of[6], 71), 0)
    out_weight = scatter_about(key_of[4], (HEAD_TOTAL * DH, D), (HEAD_TOTAL * DH) ** -0.5, 0.1875, ((0, 4),))
    out_grad = scatter_about(key_of[5], (TOKEN_TOTAL, D), 1.0, 6.0, ((0, 64), (1, 4)))
    return dict(queries=queries, raw_keys=raw_keys, values=values, write_rate=write_rate, out_weight=out_weight, out_grad=out_grad)


epsilon = 1e-06
highest = lax.Precision.HIGHEST

def unit_rows(array):
    return array * lax.rsqrt(lax.optimization_barrier(jnp.sum(array * array, -1, keepdims=True)) + epsilon)

def to_blocks(array, head_count):
    rows = array.shape[0]
    head_width = array.shape[1] // head_count
    return array.reshape(rows // BLOCK, BLOCK, head_count, head_width).transpose(2, 0, 1, 3)

def rate_blocks(decay_rate):
    rows = decay_rate.shape[0]
    head_count = decay_rate.shape[1]
    return decay_rate.reshape(rows // BLOCK, BLOCK, head_count).transpose(2, 0, 1)

def from_blocks(block_outputs):
    block_count, head_count, size, head_width = block_outputs.shape
    return block_outputs.transpose(0, 2, 1, 3).reshape(block_count * size, head_count * head_width)

def block_factors(query_blocks, key_blocks, value_blocks, rate_parts):
    unit_query = unit_rows(query_blocks)
    unit_key = unit_rows(key_blocks)
    size = unit_key.shape[-2]
    identity_block = jnp.eye(size, dtype=jnp.float32)
    key_gram = jnp.einsum('hncd,hnsd->hncs', unit_key * rate_parts[..., None], unit_key, precision=highest)
    strict_lower = jnp.tril(key_gram, -1)
    result = identity_block - strict_lower
    power_term = strict_lower
    span_done = 2
    while span_done < size:
        power_term = jnp.einsum('hnij,hnjk->hnik', power_term, power_term, precision=highest)
        result = result + jnp.einsum('hnij,hnjk->hnik', result, power_term, precision=highest)
        span_done = span_done * 2
    scaled = result * rate_parts[..., None, :]
    key_mix = jnp.einsum('hncs,hnsd->hncd', scaled, unit_key, precision=highest)
    value_mix = jnp.einsum('hncs,hnsd->hncd', scaled, value_blocks, precision=highest)
    causal_scores = jnp.tril(jnp.einsum('hncd,hnsd->hncs', unit_query, unit_key, precision=highest))
    return (unit_query, unit_key, key_mix, value_mix, causal_scores)

def run_blocks(factors, start_state):
    moved = tuple((jnp.moveaxis(member, 1, 0) for member in factors))

    def advance_block(state, pieces):
        unit_query, unit_key, key_mix, value_mix, causal_scores = pieces
        innovation = value_mix - jnp.einsum('hcd,hde->hce', key_mix, state, precision=highest)
        block_out = jnp.einsum('hcd,hde->hce', unit_query, state, precision=highest)
        block_out = block_out + jnp.einsum('hcs,hse->hce', causal_scores, innovation, precision=highest)
        state = state + jnp.einsum('hcd,hce->hde', unit_key, innovation, precision=highest)
        return (state, block_out)
    return lax.scan(advance_block, start_state, moved)

def reference(queries, raw_keys, values, write_rate, out_weight, out_grad):
    head_count = write_rate.shape[1]
    head_width = queries.shape[1] // head_count
    zero_state = jnp.zeros((head_count, head_width, head_width), jnp.float32)

    def attend(float_query, float_key, float_value, rates):
        factors = block_factors(to_blocks(float_query, head_count), to_blocks(float_key, head_count), to_blocks(float_value, head_count), rate_blocks(rates))
        final_state, block_outputs = run_blocks(factors, zero_state)
        return from_blocks(block_outputs)
    attended, pullback = jax.vjp(attend, queries.astype(jnp.float32), raw_keys.astype(jnp.float32), values.astype(jnp.float32), write_rate)
    attended_bf = attended.astype(jnp.bfloat16)
    layer_out = jnp.dot(attended_bf, out_weight, preferred_element_type=jnp.float32).astype(jnp.bfloat16)
    attended_grad = jnp.dot(out_grad, out_weight.T, preferred_element_type=jnp.float32)
    query_part, key_part, value_part, rate_grad = pullback(attended_grad)
    return (layer_out, query_part.astype(jnp.bfloat16), key_part.astype(jnp.bfloat16), value_part.astype(jnp.bfloat16), rate_grad)
```

```python
import jax
import jax.numpy as jnp
from jax import lax
from jax.sharding import PartitionSpec as P

BLOCK = 64


epsilon = 1e-06
highest = lax.Precision.HIGHEST


def unit_rows(array):
    return array * lax.rsqrt(jnp.sum(array * array, -1, keepdims=True) + epsilon)


def to_blocks(array, head_count):
    rows = array.shape[0]
    head_width = array.shape[1] // head_count
    return array.reshape(rows // BLOCK, BLOCK, head_count, head_width).transpose(2, 0, 1, 3)


def rate_blocks(decay_rate):
    rows = decay_rate.shape[0]
    head_count = decay_rate.shape[1]
    return decay_rate.reshape(rows // BLOCK, BLOCK, head_count).transpose(2, 0, 1)


def from_blocks(block_outputs):
    block_count, head_count, size, head_width = block_outputs.shape
    return block_outputs.transpose(0, 2, 1, 3).reshape(block_count * size, head_count * head_width)


def block_factors(query_blocks, key_blocks, value_blocks, rate_parts):
    unit_query = unit_rows(query_blocks)
    unit_key = unit_rows(key_blocks)
    size = unit_key.shape[-2]
    identity_block = jnp.eye(size, dtype=jnp.float32)
    key_gram = jnp.einsum(
        "hncd,hnsd->hncs", unit_key * rate_parts[..., None], unit_key, precision=highest
    )
    strict_lower = jnp.tril(key_gram, -1)
    result = identity_block - strict_lower
    power_term = strict_lower
    span_done = 2
    while span_done < size:
        power_term = jnp.einsum("hnij,hnjk->hnik", power_term, power_term, precision=highest)
        result = result + jnp.einsum("hnij,hnjk->hnik", result, power_term, precision=highest)
        span_done = span_done * 2
    scaled = result * rate_parts[..., None, :]
    key_mix = jnp.einsum("hncs,hnsd->hncd", scaled, unit_key, precision=highest)
    value_mix = jnp.einsum("hncs,hnsd->hncd", scaled, value_blocks, precision=highest)
    causal_scores = jnp.tril(jnp.einsum("hncd,hnsd->hncs", unit_query, unit_key, precision=highest))
    return (unit_query, unit_key, key_mix, value_mix, causal_scores)


def run_blocks(factors, start_state):
    moved = tuple((jnp.moveaxis(member, 1, 0) for member in factors))

    def advance_block(state, pieces):
        unit_query, unit_key, key_mix, value_mix, causal_scores = pieces
        innovation = value_mix - jnp.einsum("hcd,hde->hce", key_mix, state, precision=highest)
        block_out = jnp.einsum("hcd,hde->hce", unit_query, state, precision=highest)
        block_out = block_out + jnp.einsum(
            "hcs,hse->hce", causal_scores, innovation, precision=highest
        )
        state = state + jnp.einsum("hcd,hce->hde", unit_key, innovation, precision=highest)
        return (state, block_out)

    return lax.scan(advance_block, start_state, moved)


def mm(left, right):
    return jnp.einsum("hij,hjk->hik", left, right, precision=highest)


def scan_both(transition, offset, local_adjoint, count, axis):
    place = lax.axis_index(axis)
    fwd_map, fwd_shift = transition, offset
    bwd_map, bwd_shift = jnp.swapaxes(transition, 1, 2), local_adjoint
    step = 1
    while step < count:
        last = 2 * step >= count
        ahead = [(i, i + step) for i in range(count - step)]
        behind = [(i, i - step) for i in range(step, count)]
        if last:
            got_shift = lax.ppermute(fwd_shift, axis, ahead)
            back_shift = lax.ppermute(bwd_shift, axis, behind)
        else:
            got_map, got_shift = lax.ppermute((fwd_map, fwd_shift), axis, ahead)
            back_map, back_shift = lax.ppermute((bwd_map, bwd_shift), axis, behind)
        fwd_shift = fwd_shift + mm(fwd_map, got_shift)
        bwd_shift = bwd_shift + mm(bwd_map, back_shift)
        if not last:
            fwd_map = jnp.where(place >= step, mm(fwd_map, got_map), fwd_map)
            bwd_map = jnp.where(place + step < count, mm(bwd_map, back_map), bwd_map)
        step *= 2
    entry_state = lax.ppermute(fwd_shift, axis, [(i, i + 1) for i in range(count - 1)])
    exit_adjoint = lax.ppermute(bwd_shift, axis, [(i, i - 1) for i in range(1, count)])
    return entry_state, exit_adjoint


def head_ring(part, count, axis):
    return [part] + [
        lax.ppermute(part, axis, [(i, (i + k) % count) for i in range(count)])
        for k in range(1, count)
    ]


def make_body(seq_count, head_devices):
    def body(queries, raw_keys, values, write_rate, out_weight, out_grad):
        head_count = write_rate.shape[1]
        head_width = queries.shape[1] // head_count
        token_count = queries.shape[0]
        width = queries.shape[1]
        here = lax.axis_index("head")

        weight_cols = [lax.dynamic_slice_in_dim(out_weight, here * width, width, 1)]
        for k in range(1, head_devices):
            block = lax.dynamic_slice_in_dim(
                out_weight, ((here + k) % head_devices) * width, width, 1
            )
            weight_cols.append(
                lax.ppermute(
                    block, "head", [(i, (i + k) % head_devices) for i in range(head_devices)]
                )
            )
        weight_mine = jnp.concatenate(weight_cols, 0)

        grad_parts = head_ring(out_grad, head_devices, "head")
        weight_rows = jnp.concatenate(
            [
                lax.dynamic_slice_in_dim(
                    out_weight, ((here - k) % head_devices) * width, width, 1
                )
                for k in range(head_devices)
            ],
            1,
        )

        def factor_inputs(float_query, float_key, float_value, rates):
            return block_factors(
                to_blocks(float_query, head_count),
                to_blocks(float_key, head_count),
                to_blocks(float_value, head_count),
                rate_blocks(rates),
            )

        factors, pull_factors = jax.vjp(
            factor_inputs,
            queries.astype(jnp.float32),
            raw_keys.astype(jnp.float32),
            values.astype(jnp.float32),
            write_rate,
        )
        unit_query, unit_key, key_mix, value_mix, causal_scores = factors
        identity_heads = jnp.broadcast_to(
            jnp.eye(head_width, dtype=jnp.float32), (head_count, head_width, head_width)
        )
        zero_heads = jnp.zeros((head_count, head_width, head_width), jnp.float32)
        widened = (
            unit_query,
            unit_key,
            key_mix,
            jnp.concatenate([jnp.zeros_like(value_mix), value_mix], -1),
            causal_scores,
        )
        joined_state, joined_outputs = run_blocks(
            widened, jnp.concatenate([identity_heads, zero_heads], -1)
        )
        transition = joined_state[..., :head_width]
        offset = joined_state[..., head_width:]
        query_effect = joined_outputs[..., :head_width]
        attended_grad = lax.dot_general(
            jnp.concatenate(grad_parts, 1),
            weight_rows,
            (((1,), (1,)), ((), ())),
            preferred_element_type=jnp.float32,
        )
        grad_blocks = attended_grad.reshape(
            token_count // BLOCK, BLOCK, head_count, head_width
        ).transpose(0, 2, 1, 3)
        local_adjoint = jnp.einsum("nhcd,nhce->hde", query_effect, grad_blocks, precision=highest)
        entry_state, exit_adjoint = scan_both(transition, offset, local_adjoint, seq_count, "seq")

        def run_from_entry(factor_tuple):
            return run_blocks(factor_tuple, entry_state)

        (final_state, block_outputs), pull_run = jax.vjp(run_from_entry, factors)
        attended_bf = from_blocks(block_outputs).astype(jnp.bfloat16)
        attended_parts = head_ring(attended_bf, head_devices, "head")
        layer_out = jnp.dot(
            jnp.concatenate(attended_parts, 1), weight_mine, preferred_element_type=jnp.float32
        ).astype(jnp.bfloat16)
        factor_grads = pull_run((exit_adjoint, grad_blocks))
        query_part, key_part, value_part, rate_grad = pull_factors(factor_grads[0])
        return (
            layer_out,
            query_part.astype(jnp.bfloat16),
            key_part.astype(jnp.bfloat16),
            value_part.astype(jnp.bfloat16),
            rate_grad,
        )

    return body


def solution(mesh):
    placed = (
        P("seq", "head"),
        P("seq", "head"),
        P("seq", "head"),
        P("seq", "head"),
        P("head", None),
        P("seq", "head"),
    )
    return jax.shard_map(
        make_body(mesh.shape["seq"], mesh.shape["head"]),
        mesh=mesh,
        in_specs=placed,
        out_specs=(
            P("seq", "head"),
            P("seq", "head"),
            P("seq", "head"),
            P("seq", "head"),
            P("seq", "head"),
        ),
        check_vma=False,
    )
```

```python
import jax
import jax.numpy as jnp
from jax import lax
from jax.sharding import PartitionSpec as P

BLOCK = 64


epsilon = 1e-06
highest = lax.Precision.HIGHEST


def unit_rows(array):
    return array * lax.rsqrt(jnp.sum(array * array, -1, keepdims=True) + epsilon)


def to_blocks(array, head_count):
    rows = array.shape[0]
    head_width = array.shape[1] // head_count
    return array.reshape(rows // BLOCK, BLOCK, head_count, head_width).transpose(2, 0, 1, 3)


def rate_blocks(decay_rate):
    rows = decay_rate.shape[0]
    head_count = decay_rate.shape[1]
    return decay_rate.reshape(rows // BLOCK, BLOCK, head_count).transpose(2, 0, 1)


def from_blocks(block_outputs):
    block_count, head_count, size, head_width = block_outputs.shape
    return block_outputs.transpose(0, 2, 1, 3).reshape(block_count * size, head_count * head_width)


def block_factors(query_blocks, key_blocks, value_blocks, rate_parts):
    unit_query = unit_rows(query_blocks)
    unit_key = unit_rows(key_blocks)
    size = unit_key.shape[-2]
    identity_block = jnp.eye(size, dtype=jnp.float32)
    key_gram = jnp.einsum(
        "hncd,hnsd->hncs", unit_key * rate_parts[..., None], unit_key, precision=highest
    )
    strict_lower = jnp.tril(key_gram, -1)
    result = identity_block - strict_lower
    power_term = strict_lower
    span_done = 2
    while span_done < size:
        power_term = jnp.einsum("hnij,hnjk->hnik", power_term, power_term, precision=highest)
        result = result + jnp.einsum("hnij,hnjk->hnik", result, power_term, precision=highest)
        span_done = span_done * 2
    scaled = result * rate_parts[..., None, :]
    key_mix = jnp.einsum("hncs,hnsd->hncd", scaled, unit_key, precision=highest)
    value_mix = jnp.einsum("hncs,hnsd->hncd", scaled, value_blocks, precision=highest)
    causal_scores = jnp.tril(jnp.einsum("hncd,hnsd->hncs", unit_query, unit_key, precision=highest))
    return (unit_query, unit_key, key_mix, value_mix, causal_scores)


def run_blocks(factors, start_state):
    moved = tuple((jnp.moveaxis(member, 1, 0) for member in factors))

    def advance_block(state, pieces):
        unit_query, unit_key, key_mix, value_mix, causal_scores = pieces
        innovation = value_mix - jnp.einsum("hcd,hde->hce", key_mix, state, precision=highest)
        block_out = jnp.einsum("hcd,hde->hce", unit_query, state, precision=highest)
        block_out = block_out + jnp.einsum(
            "hcs,hse->hce", causal_scores, innovation, precision=highest
        )
        state = state + jnp.einsum("hcd,hce->hde", unit_key, innovation, precision=highest)
        return (state, block_out)

    return lax.scan(advance_block, start_state, moved)


def mm(left, right):
    return jnp.einsum("hij,hjk->hik", left, right, precision=highest)


def mm_t(left, right):
    return jnp.einsum("hji,hjk->hik", left, right, precision=highest)


def scan_both(transition, offset, local_adjoint, count, axis):
    place = lax.axis_index(axis)
    width = transition.shape[-1]
    total_map, total_shift, total_adjoint = transition, offset, local_adjoint
    entry_map = entry_state = exit_map = exit_adjoint = None
    step = 1
    while step < count:
        last = 2 * step >= count
        pairs = [(i, i ^ step) for i in range(count)]
        upper = (place & step) != 0
        if last:
            sent = jnp.concatenate([total_shift, total_adjoint], -1)
        else:
            sent = jnp.concatenate([total_map, total_shift, total_adjoint], -1)
        got = lax.ppermute(sent, axis, pairs)
        mine = sent
        low = jnp.where(upper, got, mine)
        high = jnp.where(upper, mine, got)
        if last:
            low_shift = low[..., :width]
            high_adjoint = high[..., width:]
        else:
            low_map, low_shift = low[..., :width], low[..., width : 2 * width]
            high_map, high_adjoint = high[..., :width], high[..., 2 * width :]
        if entry_map is None:
            entry_state = jnp.where(upper, low_shift, jnp.zeros_like(low_shift))
            exit_adjoint = jnp.where(upper, jnp.zeros_like(high_adjoint), high_adjoint)
            if not last:
                eye = jnp.broadcast_to(jnp.eye(width, dtype=jnp.float32), low_map.shape)
                entry_map = jnp.where(upper, low_map, eye)
                exit_map = jnp.where(upper, eye, jnp.swapaxes(high_map, 1, 2))
        else:
            entry_state = jnp.where(upper, entry_state + mm(entry_map, low_shift), entry_state)
            exit_adjoint = jnp.where(upper, exit_adjoint, exit_adjoint + mm(exit_map, high_adjoint))
            if not last:
                entry_map = jnp.where(upper, mm(entry_map, low_map), entry_map)
                exit_map = jnp.where(
                    upper, exit_map, jnp.einsum("hij,hkj->hik", exit_map, high_map, precision=highest)
                )
        if not last:
            joined = mm(high_map, jnp.concatenate([low_map, low_shift], -1))
            total_map = joined[..., :width]
            total_shift = joined[..., width:] + high[..., width : 2 * width]
            total_adjoint = mm_t(low_map, high_adjoint) + low[..., 2 * width :]
        step *= 2
    return entry_state, exit_adjoint


def head_ring(part, count, axis):
    return [part] + [
        lax.ppermute(part, axis, [(i, (i + k) % count) for i in range(count)])
        for k in range(1, count)
    ]


def make_body(seq_count, head_devices):
    def body(queries, raw_keys, values, write_rate, out_weight, out_grad):
        head_count = write_rate.shape[1]
        head_width = queries.shape[1] // head_count
        token_count = queries.shape[0]
        width = queries.shape[1]
        here = lax.axis_index("head")

        weight_cols = [lax.dynamic_slice_in_dim(out_weight, here * width, width, 1)]
        for k in range(1, head_devices):
            block = lax.dynamic_slice_in_dim(
                out_weight, ((here + k) % head_devices) * width, width, 1
            )
            weight_cols.append(
                lax.ppermute(
                    block, "head", [(i, (i + k) % head_devices) for i in range(head_devices)]
                )
            )
        weight_mine = jnp.concatenate(weight_cols, 0)

        grad_parts = head_ring(out_grad, head_devices, "head")
        weight_rows = jnp.concatenate(
            [
                lax.dynamic_slice_in_dim(
                    out_weight, ((here - k) % head_devices) * width, width, 1
                )
                for k in range(head_devices)
            ],
            1,
        )

        def factor_inputs(float_query, float_key, float_value, rates):
            return block_factors(
                to_blocks(float_query, head_count),
                to_blocks(float_key, head_count),
                to_blocks(float_value, head_count),
                rate_blocks(rates),
            )

        factors, pull_factors = jax.vjp(
            factor_inputs,
            queries.astype(jnp.float32),
            raw_keys.astype(jnp.float32),
            values.astype(jnp.float32),
            write_rate,
        )
        unit_query, unit_key, key_mix, value_mix, causal_scores = factors
        identity_heads = jnp.broadcast_to(
            jnp.eye(head_width, dtype=jnp.float32), (head_count, head_width, head_width)
        )
        zero_heads = jnp.zeros((head_count, head_width, head_width), jnp.float32)
        widened = (
            unit_query,
            unit_key,
            key_mix,
            jnp.concatenate([jnp.zeros_like(value_mix), value_mix], -1),
            causal_scores,
        )
        joined_state, joined_outputs = run_blocks(
            widened, jnp.concatenate([identity_heads, zero_heads], -1)
        )
        transition = joined_state[..., :head_width]
        offset = joined_state[..., head_width:]
        query_effect = joined_outputs[..., :head_width]
        attended_grad = lax.dot_general(
            jnp.concatenate(grad_parts, 1),
            weight_rows,
            (((1,), (1,)), ((), ())),
            preferred_element_type=jnp.float32,
        )
        grad_blocks = attended_grad.reshape(
            token_count // BLOCK, BLOCK, head_count, head_width
        ).transpose(0, 2, 1, 3)
        local_adjoint = jnp.einsum("nhcd,nhce->hde", query_effect, grad_blocks, precision=highest)
        entry_state, exit_adjoint = scan_both(transition, offset, local_adjoint, seq_count, "seq")

        def run_from_entry(factor_tuple):
            return run_blocks(factor_tuple, entry_state)

        (final_state, block_outputs), pull_run = jax.vjp(run_from_entry, factors)
        attended_bf = from_blocks(block_outputs).astype(jnp.bfloat16)
        attended_parts = head_ring(attended_bf, head_devices, "head")
        layer_out = jnp.dot(
            jnp.concatenate(attended_parts, 1), weight_mine, preferred_element_type=jnp.float32
        ).astype(jnp.bfloat16)
        factor_grads = pull_run((exit_adjoint, grad_blocks))
        query_part, key_part, value_part, rate_grad = pull_factors(factor_grads[0])
        return (
            layer_out,
            query_part.astype(jnp.bfloat16),
            key_part.astype(jnp.bfloat16),
            value_part.astype(jnp.bfloat16),
            rate_grad,
        )

    return body


def solution(mesh):
    placed = (
        P("seq", "head"),
        P("seq", "head"),
        P("seq", "head"),
        P("seq", "head"),
        P("head", None),
        P("seq", "head"),
    )
    return jax.shard_map(
        make_body(mesh.shape["seq"], mesh.shape["head"]),
        mesh=mesh,
        in_specs=placed,
        out_specs=(
            P("seq", "head"),
            P("seq", "head"),
            P("seq", "head"),
            P("seq", "head"),
            P("seq", "head"),
        ),
        check_vma=False,
    )
```

```python
import jax
import jax.numpy as jnp
from jax import lax
from jax.sharding import PartitionSpec as P

BLOCK = 64


epsilon = 1e-06
highest = lax.Precision.HIGHEST


def unit_rows(array):
    return array * lax.rsqrt(jnp.sum(array * array, -1, keepdims=True) + epsilon)


def to_blocks(array, head_count):
    rows = array.shape[0]
    head_width = array.shape[1] // head_count
    return array.reshape(rows // BLOCK, BLOCK, head_count, head_width).transpose(2, 0, 1, 3)


def rate_blocks(decay_rate):
    rows = decay_rate.shape[0]
    head_count = decay_rate.shape[1]
    return decay_rate.reshape(rows // BLOCK, BLOCK, head_count).transpose(2, 0, 1)


def from_blocks(block_outputs):
    block_count, head_count, size, head_width = block_outputs.shape
    return block_outputs.transpose(0, 2, 1, 3).reshape(block_count * size, head_count * head_width)


def block_factors(query_blocks, key_blocks, value_blocks, rate_parts):
    unit_query = unit_rows(query_blocks)
    unit_key = unit_rows(key_blocks)
    size = unit_key.shape[-2]
    identity_block = jnp.eye(size, dtype=jnp.float32)
    key_gram = jnp.einsum(
        "hncd,hnsd->hncs", unit_key * rate_parts[..., None], unit_key, precision=highest
    )
    strict_lower = jnp.tril(key_gram, -1)
    result = identity_block - strict_lower
    power_term = strict_lower
    span_done = 2
    while span_done < size:
        power_term = jnp.einsum("hnij,hnjk->hnik", power_term, power_term, precision=highest)
        result = result + jnp.einsum("hnij,hnjk->hnik", result, power_term, precision=highest)
        span_done = span_done * 2
    scaled = result * rate_parts[..., None, :]
    key_mix = jnp.einsum("hncs,hnsd->hncd", scaled, unit_key, precision=highest)
    value_mix = jnp.einsum("hncs,hnsd->hncd", scaled, value_blocks, precision=highest)
    causal_scores = jnp.tril(jnp.einsum("hncd,hnsd->hncs", unit_query, unit_key, precision=highest))
    return (unit_query, unit_key, key_mix, value_mix, causal_scores)


def run_blocks(factors, start_state):
    moved = tuple((jnp.moveaxis(member, 1, 0) for member in factors))

    def advance_block(state, pieces):
        unit_query, unit_key, key_mix, value_mix, causal_scores = pieces
        innovation = value_mix - jnp.einsum("hcd,hde->hce", key_mix, state, precision=highest)
        block_out = jnp.einsum("hcd,hde->hce", unit_query, state, precision=highest)
        block_out = block_out + jnp.einsum(
            "hcs,hse->hce", causal_scores, innovation, precision=highest
        )
        state = state + jnp.einsum("hcd,hce->hde", unit_key, innovation, precision=highest)
        return (state, block_out)

    return lax.scan(advance_block, start_state, moved)


def mm(left, right):
    return jnp.einsum("hij,hjk->hik", left, right, precision=highest)


def mm_t(left, right):
    return jnp.einsum("hji,hjk->hik", left, right, precision=highest)


def pick_head(array, index):
    return lax.dynamic_slice_in_dim(array, index, 1, 0)


def scan_both(transition, offset, local_adjoint, count, axis):
    place = lax.axis_index(axis)
    width = transition.shape[-1]
    core = place % 2
    own = jnp.concatenate([transition, offset, local_adjoint], -1)
    got = lax.ppermute(pick_head(own, 1 - core), axis, [(i, i ^ 1) for i in range(count)])
    mine = pick_head(own, core)
    second = core == 1
    low = jnp.where(second, got, mine)
    high = jnp.where(second, mine, got)
    core_low, core_high = low, high
    joined = mm(high[..., :width], jnp.concatenate([low[..., :width], low[..., width : 2 * width]], -1))
    total_map = joined[..., :width]
    total_shift = joined[..., width:] + high[..., width : 2 * width]
    total_adjoint = mm_t(low[..., :width], high[..., 2 * width :]) + low[..., 2 * width :]
    entry_map = entry_state = exit_map = exit_adjoint = None
    step = 2
    while step < count:
        last = 2 * step >= count
        pairs = [(i, i ^ step) for i in range(count)]
        upper = (place & step) != 0
        if last:
            sent = jnp.concatenate([total_shift, total_adjoint], -1)
        else:
            sent = jnp.concatenate([total_map, total_shift, total_adjoint], -1)
        got = lax.ppermute(sent, axis, pairs)
        low = jnp.where(upper, got, sent)
        high = jnp.where(upper, sent, got)
        if last:
            low_shift = low[..., :width]
            high_adjoint = high[..., width:]
        else:
            low_map, low_shift = low[..., :width], low[..., width : 2 * width]
            high_map, high_adjoint = high[..., :width], high[..., 2 * width :]
        if entry_map is None:
            entry_state = jnp.where(upper, low_shift, jnp.zeros_like(low_shift))
            exit_adjoint = jnp.where(upper, jnp.zeros_like(high_adjoint), high_adjoint)
            if not last:
                eye = jnp.broadcast_to(jnp.eye(width, dtype=jnp.float32), low_map.shape)
                entry_map = jnp.where(upper, low_map, eye)
                exit_map = jnp.where(upper, eye, jnp.swapaxes(high_map, 1, 2))
        else:
            entry_state = jnp.where(upper, entry_state + mm(entry_map, low_shift), entry_state)
            exit_adjoint = jnp.where(upper, exit_adjoint, exit_adjoint + mm(exit_map, high_adjoint))
            if not last:
                entry_map = jnp.where(upper, mm(entry_map, low_map), entry_map)
                exit_map = jnp.where(
                    upper, exit_map, jnp.einsum("hij,hkj->hik", exit_map, high_map, precision=highest)
                )
        if not last:
            joined = mm(high_map, jnp.concatenate([low_map, low_shift], -1))
            total_map = joined[..., :width]
            total_shift = joined[..., width:] + high[..., width : 2 * width]
            total_adjoint = mm_t(low_map, high_adjoint) + low[..., 2 * width :]
        step *= 2
    if entry_state is None:
        entry_state = jnp.zeros_like(total_shift)
        exit_adjoint = jnp.zeros_like(total_adjoint)
    entry_second = mm(core_low[..., :width], entry_state) + core_low[..., width : 2 * width]
    exit_first = mm_t(core_high[..., :width], exit_adjoint) + core_high[..., 2 * width :]
    mine = jnp.concatenate(
        [jnp.where(second, entry_second, entry_state), jnp.where(second, exit_adjoint, exit_first)], -1
    )
    other = jnp.concatenate(
        [jnp.where(second, entry_state, entry_second), jnp.where(second, exit_first, exit_adjoint)], -1
    )
    back = lax.ppermute(other, axis, [(i, i ^ 1) for i in range(count)])
    both = jnp.where(second, jnp.concatenate([back, mine], 0), jnp.concatenate([mine, back], 0))
    return both[..., :width], both[..., width:]


def head_ring(part, count, axis):
    return [part] + [
        lax.ppermute(part, axis, [(i, (i + k) % count) for i in range(count)])
        for k in range(1, count)
    ]


def make_body(seq_count, head_devices):
    def body(queries, raw_keys, values, write_rate, out_weight, out_grad):
        head_count = write_rate.shape[1]
        head_width = queries.shape[1] // head_count
        token_count = queries.shape[0]
        width = queries.shape[1]
        here = lax.axis_index("head")

        weight_cols = [lax.dynamic_slice_in_dim(out_weight, here * width, width, 1)]
        for k in range(1, head_devices):
            block = lax.dynamic_slice_in_dim(
                out_weight, ((here + k) % head_devices) * width, width, 1
            )
            weight_cols.append(
                lax.ppermute(
                    block, "head", [(i, (i + k) % head_devices) for i in range(head_devices)]
                )
            )
        weight_mine = jnp.concatenate(weight_cols, 0)

        grad_parts = head_ring(out_grad, head_devices, "head")
        weight_rows = jnp.concatenate(
            [
                lax.dynamic_slice_in_dim(
                    out_weight, ((here - k) % head_devices) * width, width, 1
                )
                for k in range(head_devices)
            ],
            1,
        )

        def factor_inputs(float_query, float_key, float_value, rates):
            return block_factors(
                to_blocks(float_query, head_count),
                to_blocks(float_key, head_count),
                to_blocks(float_value, head_count),
                rate_blocks(rates),
            )

        factors, pull_factors = jax.vjp(
            factor_inputs,
            queries.astype(jnp.float32),
            raw_keys.astype(jnp.float32),
            values.astype(jnp.float32),
            write_rate,
        )
        unit_query, unit_key, key_mix, value_mix, causal_scores = factors
        identity_heads = jnp.broadcast_to(
            jnp.eye(head_width, dtype=jnp.float32), (head_count, head_width, head_width)
        )
        zero_heads = jnp.zeros((head_count, head_width, head_width), jnp.float32)
        widened = (
            unit_query,
            unit_key,
            key_mix,
            jnp.concatenate([jnp.zeros_like(value_mix), value_mix], -1),
            causal_scores,
        )
        joined_state, joined_outputs = run_blocks(
            widened, jnp.concatenate([identity_heads, zero_heads], -1)
        )
        transition = joined_state[..., :head_width]
        offset = joined_state[..., head_width:]
        query_effect = joined_outputs[..., :head_width]
        attended_grad = lax.dot_general(
            jnp.concatenate(grad_parts, 1),
            weight_rows,
            (((1,), (1,)), ((), ())),
            preferred_element_type=jnp.float32,
        )
        grad_blocks = attended_grad.reshape(
            token_count // BLOCK, BLOCK, head_count, head_width
        ).transpose(0, 2, 1, 3)
        local_adjoint = jnp.einsum("nhcd,nhce->hde", query_effect, grad_blocks, precision=highest)
        entry_state, exit_adjoint = scan_both(transition, offset, local_adjoint, seq_count, "seq")

        def run_from_entry(factor_tuple):
            return run_blocks(factor_tuple, entry_state)

        (final_state, block_outputs), pull_run = jax.vjp(run_from_entry, factors)
        attended_bf = from_blocks(block_outputs).astype(jnp.bfloat16)
        attended_parts = head_ring(attended_bf, head_devices, "head")
        layer_out = jnp.dot(
            jnp.concatenate(attended_parts, 1), weight_mine, preferred_element_type=jnp.float32
        ).astype(jnp.bfloat16)
        factor_grads = pull_run((exit_adjoint, grad_blocks))
        query_part, key_part, value_part, rate_grad = pull_factors(factor_grads[0])
        return (
            layer_out,
            query_part.astype(jnp.bfloat16),
            key_part.astype(jnp.bfloat16),
            value_part.astype(jnp.bfloat16),
            rate_grad,
        )

    return body


def solution(mesh):
    placed = (
        P("seq", "head"),
        P("seq", "head"),
        P("seq", "head"),
        P("seq", "head"),
        P("head", None),
        P("seq", "head"),
    )
    return jax.shard_map(
        make_body(mesh.shape["seq"], mesh.shape["head"]),
        mesh=mesh,
        in_specs=placed,
        out_specs=(
            P("seq", "head"),
            P("seq", "head"),
            P("seq", "head"),
            P("seq", "head"),
            P("seq", "head"),
        ),
        check_vma=False,
    )
```

```python
import jax
import jax.numpy as jnp
from jax import lax
from jax.sharding import PartitionSpec as P

BLOCK = 64


epsilon = 1e-06
highest = lax.Precision.HIGHEST


def unit_rows(array):
    return array * lax.rsqrt(jnp.sum(array * array, -1, keepdims=True) + epsilon)


def to_blocks(array, head_count):
    rows = array.shape[0]
    head_width = array.shape[1] // head_count
    return array.reshape(rows // BLOCK, BLOCK, head_count, head_width).transpose(2, 0, 1, 3)


def rate_blocks(decay_rate):
    rows = decay_rate.shape[0]
    head_count = decay_rate.shape[1]
    return decay_rate.reshape(rows // BLOCK, BLOCK, head_count).transpose(2, 0, 1)


def from_blocks(block_outputs):
    block_count, head_count, size, head_width = block_outputs.shape
    return block_outputs.transpose(0, 2, 1, 3).reshape(block_count * size, head_count * head_width)


@jax.custom_vjp
def unit_lower_inverse(strict_lower):
    return unit_lower_inverse_fwd(strict_lower)[0]


def unit_lower_inverse_fwd(strict_lower):
    size = strict_lower.shape[-1]
    result = jnp.eye(size, dtype=jnp.float32) - strict_lower
    power_term = strict_lower
    span_done = 2
    while span_done < size:
        power_term = jnp.einsum("hnij,hnjk->hnik", power_term, power_term, precision=highest)
        result = result + jnp.einsum("hnij,hnjk->hnik", result, power_term, precision=highest)
        span_done = span_done * 2
    return result, result


def unit_lower_inverse_bwd(result, grad):
    inner = jnp.einsum("hnji,hnjk->hnik", result, grad, precision=highest)
    outer = jnp.einsum("hnij,hnkj->hnik", inner, result, precision=highest)
    return (jnp.tril(-outer, -1),)


unit_lower_inverse.defvjp(unit_lower_inverse_fwd, unit_lower_inverse_bwd)


def block_factors(query_blocks, key_blocks, value_blocks, rate_parts):
    unit_query = unit_rows(query_blocks)
    unit_key = unit_rows(key_blocks)
    key_gram = jnp.einsum(
        "hncd,hnsd->hncs", unit_key * rate_parts[..., None], unit_key, precision=highest
    )
    strict_lower = jnp.tril(key_gram, -1)
    result = unit_lower_inverse(strict_lower)
    scaled = result * rate_parts[..., None, :]
    key_mix = jnp.einsum("hncs,hnsd->hncd", scaled, unit_key, precision=highest)
    value_mix = jnp.einsum("hncs,hnsd->hncd", scaled, value_blocks, precision=highest)
    causal_scores = jnp.tril(jnp.einsum("hncd,hnsd->hncs", unit_query, unit_key, precision=highest))
    return (unit_query, unit_key, key_mix, value_mix, causal_scores)


def run_blocks(factors, start_state):
    moved = tuple((jnp.moveaxis(member, 1, 0) for member in factors))

    def advance_block(state, pieces):
        unit_query, unit_key, key_mix, value_mix, causal_scores = pieces
        innovation = value_mix - jnp.einsum("hcd,hde->hce", key_mix, state, precision=highest)
        block_out = jnp.einsum("hcd,hde->hce", unit_query, state, precision=highest)
        block_out = block_out + jnp.einsum(
            "hcs,hse->hce", causal_scores, innovation, precision=highest
        )
        state = state + jnp.einsum("hcd,hce->hde", unit_key, innovation, precision=highest)
        return (state, block_out)

    return lax.scan(advance_block, start_state, moved)


def mm(left, right):
    return jnp.einsum("hij,hjk->hik", left, right, precision=highest)


def mm_t(left, right):
    return jnp.einsum("hji,hjk->hik", left, right, precision=highest)


def pick_head(array, index):
    return lax.dynamic_slice_in_dim(array, index, 1, 0)


def scan_both(transition, offset, local_adjoint, count, axis):
    place = lax.axis_index(axis)
    width = transition.shape[-1]
    core = place % 2
    own = jnp.concatenate([transition, offset, local_adjoint], -1)
    got = lax.ppermute(pick_head(own, 1 - core), axis, [(i, i ^ 1) for i in range(count)])
    mine = pick_head(own, core)
    second = core == 1
    low = jnp.where(second, got, mine)
    high = jnp.where(second, mine, got)
    core_low, core_high = low, high
    joined = mm(high[..., :width], jnp.concatenate([low[..., :width], low[..., width : 2 * width]], -1))
    total_map = joined[..., :width]
    total_shift = joined[..., width:] + high[..., width : 2 * width]
    total_adjoint = mm_t(low[..., :width], high[..., 2 * width :]) + low[..., 2 * width :]
    entry_map = entry_state = exit_map = exit_adjoint = None
    step = 2
    while step < count:
        last = 2 * step >= count
        pairs = [(i, i ^ step) for i in range(count)]
        upper = (place & step) != 0
        if last:
            sent = jnp.concatenate([total_shift, total_adjoint], -1)
        else:
            sent = jnp.concatenate([total_map, total_shift, total_adjoint], -1)
        got = lax.ppermute(sent, axis, pairs)
        low = jnp.where(upper, got, sent)
        high = jnp.where(upper, sent, got)
        if last:
            low_shift = low[..., :width]
            high_adjoint = high[..., width:]
        else:
            low_map, low_shift = low[..., :width], low[..., width : 2 * width]
            high_map, high_adjoint = high[..., :width], high[..., 2 * width :]
        if entry_map is None:
            entry_state = jnp.where(upper, low_shift, jnp.zeros_like(low_shift))
            exit_adjoint = jnp.where(upper, jnp.zeros_like(high_adjoint), high_adjoint)
            if not last:
                eye = jnp.broadcast_to(jnp.eye(width, dtype=jnp.float32), low_map.shape)
                entry_map = jnp.where(upper, low_map, eye)
                exit_map = jnp.where(upper, eye, jnp.swapaxes(high_map, 1, 2))
        else:
            entry_state = jnp.where(upper, entry_state + mm(entry_map, low_shift), entry_state)
            exit_adjoint = jnp.where(upper, exit_adjoint, exit_adjoint + mm(exit_map, high_adjoint))
            if not last:
                entry_map = jnp.where(upper, mm(entry_map, low_map), entry_map)
                exit_map = jnp.where(
                    upper, exit_map, jnp.einsum("hij,hkj->hik", exit_map, high_map, precision=highest)
                )
        if not last:
            joined = mm(high_map, jnp.concatenate([low_map, low_shift], -1))
            total_map = joined[..., :width]
            total_shift = joined[..., width:] + high[..., width : 2 * width]
            total_adjoint = mm_t(low_map, high_adjoint) + low[..., 2 * width :]
        step *= 2
    if entry_state is None:
        entry_state = jnp.zeros_like(total_shift)
        exit_adjoint = jnp.zeros_like(total_adjoint)
    entry_second = mm(core_low[..., :width], entry_state) + core_low[..., width : 2 * width]
    exit_first = mm_t(core_high[..., :width], exit_adjoint) + core_high[..., 2 * width :]
    mine = jnp.concatenate(
        [jnp.where(second, entry_second, entry_state), jnp.where(second, exit_adjoint, exit_first)], -1
    )
    other = jnp.concatenate(
        [jnp.where(second, entry_state, entry_second), jnp.where(second, exit_first, exit_adjoint)], -1
    )
    back = lax.ppermute(other, axis, [(i, i ^ 1) for i in range(count)])
    both = jnp.where(second, jnp.concatenate([back, mine], 0), jnp.concatenate([mine, back], 0))
    return both[..., :width], both[..., width:]


def head_ring(part, count, axis):
    return [part] + [
        lax.ppermute(part, axis, [(i, (i + k) % count) for i in range(count)])
        for k in range(1, count)
    ]


def make_body(seq_count, head_devices):
    def body(queries, raw_keys, values, write_rate, out_weight, out_grad):
        head_count = write_rate.shape[1]
        head_width = queries.shape[1] // head_count
        token_count = queries.shape[0]
        width = queries.shape[1]
        here = lax.axis_index("head")

        rows = out_grad.shape[0]
        weight_cols = [lax.dynamic_slice_in_dim(out_weight, here * width, width, 1)]
        grad_parts = [out_grad]
        for k in range(1, head_devices):
            block = lax.dynamic_slice_in_dim(
                out_weight, ((here + k) % head_devices) * width, width, 1
            )
            moved = lax.ppermute(
                jnp.concatenate([out_grad, block], 0),
                "head",
                [(i, (i + k) % head_devices) for i in range(head_devices)],
            )
            grad_parts.append(moved[:rows])
            weight_cols.append(moved[rows:])
        weight_mine = jnp.concatenate(weight_cols, 0)

        weight_rows = jnp.concatenate(
            [
                lax.dynamic_slice_in_dim(
                    out_weight, ((here - k) % head_devices) * width, width, 1
                )
                for k in range(head_devices)
            ],
            1,
        )

        def factor_inputs(float_query, float_key, float_value, rates):
            return block_factors(
                to_blocks(float_query, head_count),
                to_blocks(float_key, head_count),
                to_blocks(float_value, head_count),
                rate_blocks(rates),
            )

        factors, pull_factors = jax.vjp(
            factor_inputs,
            queries.astype(jnp.float32),
            raw_keys.astype(jnp.float32),
            values.astype(jnp.float32),
            write_rate,
        )
        unit_query, unit_key, key_mix, value_mix, causal_scores = factors
        identity_heads = jnp.broadcast_to(
            jnp.eye(head_width, dtype=jnp.float32), (head_count, head_width, head_width)
        )
        zero_heads = jnp.zeros((head_count, head_width, head_width), jnp.float32)
        widened = (
            unit_query,
            unit_key,
            key_mix,
            jnp.concatenate([jnp.zeros_like(value_mix), value_mix], -1),
            causal_scores,
        )
        joined_state, joined_outputs = run_blocks(
            widened, jnp.concatenate([identity_heads, zero_heads], -1)
        )
        transition = joined_state[..., :head_width]
        offset = joined_state[..., head_width:]
        query_effect = joined_outputs[..., :head_width]
        attended_grad = lax.dot_general(
            jnp.concatenate(grad_parts, 1),
            weight_rows,
            (((1,), (1,)), ((), ())),
            preferred_element_type=jnp.float32,
        )
        grad_blocks = attended_grad.reshape(
            token_count // BLOCK, BLOCK, head_count, head_width
        ).transpose(0, 2, 1, 3)
        local_adjoint = jnp.einsum("nhcd,nhce->hde", query_effect, grad_blocks, precision=highest)
        entry_state, exit_adjoint = scan_both(transition, offset, local_adjoint, seq_count, "seq")

        def run_from_entry(factor_tuple):
            return run_blocks(factor_tuple, entry_state)

        (final_state, block_outputs), pull_run = jax.vjp(run_from_entry, factors)
        attended_bf = from_blocks(block_outputs).astype(jnp.bfloat16)
        attended_parts = head_ring(attended_bf, head_devices, "head")
        layer_out = jnp.dot(
            jnp.concatenate(attended_parts, 1), weight_mine, preferred_element_type=jnp.float32
        ).astype(jnp.bfloat16)
        factor_grads = pull_run((exit_adjoint, grad_blocks))
        query_part, key_part, value_part, rate_grad = pull_factors(factor_grads[0])
        return (
            layer_out,
            query_part.astype(jnp.bfloat16),
            key_part.astype(jnp.bfloat16),
            value_part.astype(jnp.bfloat16),
            rate_grad,
        )

    return body


def solution(mesh):
    placed = (
        P("seq", "head"),
        P("seq", "head"),
        P("seq", "head"),
        P("seq", "head"),
        P("head", None),
        P("seq", "head"),
    )
    return jax.shard_map(
        make_body(mesh.shape["seq"], mesh.shape["head"]),
        mesh=mesh,
        in_specs=placed,
        out_specs=(
            P("seq", "head"),
            P("seq", "head"),
            P("seq", "head"),
            P("seq", "head"),
            P("seq", "head"),
        ),
        check_vma=False,
    )
```

```python
import jax
import jax.numpy as jnp
from jax import lax
from jax.sharding import PartitionSpec as P

BLOCK = 64


epsilon = 1e-06
highest = lax.Precision.HIGHEST


def unit_rows(array):
    return array * lax.rsqrt(jnp.sum(array * array, -1, keepdims=True) + epsilon)


def to_blocks(array, head_count):
    rows = array.shape[0]
    head_width = array.shape[1] // head_count
    return array.reshape(rows // BLOCK, BLOCK, head_count, head_width).transpose(2, 0, 1, 3)


def rate_blocks(decay_rate):
    rows = decay_rate.shape[0]
    head_count = decay_rate.shape[1]
    return decay_rate.reshape(rows // BLOCK, BLOCK, head_count).transpose(2, 0, 1)


def from_blocks(block_outputs):
    block_count, head_count, size, head_width = block_outputs.shape
    return block_outputs.transpose(0, 2, 1, 3).reshape(block_count * size, head_count * head_width)


@jax.custom_vjp
def unit_lower_inverse(strict_lower):
    return unit_lower_inverse_fwd(strict_lower)[0]


def unit_lower_inverse_fwd(strict_lower):
    size = strict_lower.shape[-1]
    result = jnp.eye(size, dtype=jnp.float32) - strict_lower
    power_term = strict_lower
    span_done = 2
    while span_done < size:
        power_term = jnp.einsum("hnij,hnjk->hnik", power_term, power_term, precision=highest)
        result = result + jnp.einsum("hnij,hnjk->hnik", result, power_term, precision=highest)
        span_done = span_done * 2
    return result, result


def unit_lower_inverse_bwd(result, grad):
    inner = jnp.einsum("hnji,hnjk->hnik", result, grad, precision=highest)
    outer = jnp.einsum("hnij,hnkj->hnik", inner, result, precision=highest)
    return (jnp.tril(-outer, -1),)


unit_lower_inverse.defvjp(unit_lower_inverse_fwd, unit_lower_inverse_bwd)


def block_factors(query_blocks, key_blocks, value_blocks, rate_parts):
    unit_query = unit_rows(query_blocks)
    unit_key = unit_rows(key_blocks)
    key_gram = jnp.einsum(
        "hncd,hnsd->hncs", unit_key * rate_parts[..., None], unit_key, precision=highest
    )
    strict_lower = jnp.tril(key_gram, -1)
    result = unit_lower_inverse(strict_lower)
    scaled = result * rate_parts[..., None, :]
    key_mix = jnp.einsum("hncs,hnsd->hncd", scaled, unit_key, precision=highest)
    value_mix = jnp.einsum("hncs,hnsd->hncd", scaled, value_blocks, precision=highest)
    causal_scores = jnp.tril(jnp.einsum("hncd,hnsd->hncs", unit_query, unit_key, precision=highest))
    return (unit_query, unit_key, key_mix, value_mix, causal_scores)


def run_blocks(factors, start_state):
    moved = tuple((jnp.moveaxis(member, 1, 0) for member in factors))

    def advance_block(state, pieces):
        unit_query, unit_key, key_mix, value_mix, causal_scores = pieces
        innovation = value_mix - jnp.einsum("hcd,hde->hce", key_mix, state, precision=highest)
        block_out = jnp.einsum("hcd,hde->hce", unit_query, state, precision=highest)
        block_out = block_out + jnp.einsum(
            "hcs,hse->hce", causal_scores, innovation, precision=highest
        )
        state = state + jnp.einsum("hcd,hce->hde", unit_key, innovation, precision=highest)
        return (state, block_out)

    return lax.scan(advance_block, start_state, moved, unroll=True)


def mm(left, right):
    return jnp.einsum("hij,hjk->hik", left, right, precision=highest)


def mm_t(left, right):
    return jnp.einsum("hji,hjk->hik", left, right, precision=highest)


def pick_head(array, index):
    return lax.dynamic_slice_in_dim(array, index, 1, 0)


def scan_both(transition, offset, local_adjoint, count, axis):
    place = lax.axis_index(axis)
    width = transition.shape[-1]
    core = place % 2
    own = jnp.concatenate([transition, offset, local_adjoint], -1)
    got = lax.ppermute(pick_head(own, 1 - core), axis, [(i, i ^ 1) for i in range(count)])
    mine = pick_head(own, core)
    second = core == 1
    low = jnp.where(second, got, mine)
    high = jnp.where(second, mine, got)
    core_low, core_high = low, high
    joined = mm(high[..., :width], jnp.concatenate([low[..., :width], low[..., width : 2 * width]], -1))
    total_map = joined[..., :width]
    total_shift = joined[..., width:] + high[..., width : 2 * width]
    total_adjoint = mm_t(low[..., :width], high[..., 2 * width :]) + low[..., 2 * width :]
    entry_map = entry_state = exit_map = exit_adjoint = None
    step = 2
    while step < count:
        last = 2 * step >= count
        pairs = [(i, i ^ step) for i in range(count)]
        upper = (place & step) != 0
        if last:
            sent = jnp.concatenate([total_shift, total_adjoint], -1)
        else:
            sent = jnp.concatenate([total_map, total_shift, total_adjoint], -1)
        got = lax.ppermute(sent, axis, pairs)
        low = jnp.where(upper, got, sent)
        high = jnp.where(upper, sent, got)
        if last:
            low_shift = low[..., :width]
            high_adjoint = high[..., width:]
        else:
            low_map, low_shift = low[..., :width], low[..., width : 2 * width]
            high_map, high_adjoint = high[..., :width], high[..., 2 * width :]
        if entry_map is None:
            entry_state = jnp.where(upper, low_shift, jnp.zeros_like(low_shift))
            exit_adjoint = jnp.where(upper, jnp.zeros_like(high_adjoint), high_adjoint)
            if not last:
                eye = jnp.broadcast_to(jnp.eye(width, dtype=jnp.float32), low_map.shape)
                entry_map = jnp.where(upper, low_map, eye)
                exit_map = jnp.where(upper, eye, jnp.swapaxes(high_map, 1, 2))
        else:
            entry_state = jnp.where(upper, entry_state + mm(entry_map, low_shift), entry_state)
            exit_adjoint = jnp.where(upper, exit_adjoint, exit_adjoint + mm(exit_map, high_adjoint))
            if not last:
                entry_map = jnp.where(upper, mm(entry_map, low_map), entry_map)
                exit_map = jnp.where(
                    upper, exit_map, jnp.einsum("hij,hkj->hik", exit_map, high_map, precision=highest)
                )
        if not last:
            joined = mm(high_map, jnp.concatenate([low_map, low_shift], -1))
            total_map = joined[..., :width]
            total_shift = joined[..., width:] + high[..., width : 2 * width]
            total_adjoint = mm_t(low_map, high_adjoint) + low[..., 2 * width :]
        step *= 2
    if entry_state is None:
        entry_state = jnp.zeros_like(total_shift)
        exit_adjoint = jnp.zeros_like(total_adjoint)
    entry_second = mm(core_low[..., :width], entry_state) + core_low[..., width : 2 * width]
    exit_first = mm_t(core_high[..., :width], exit_adjoint) + core_high[..., 2 * width :]
    mine = jnp.concatenate(
        [jnp.where(second, entry_second, entry_state), jnp.where(second, exit_adjoint, exit_first)], -1
    )
    other = jnp.concatenate(
        [jnp.where(second, entry_state, entry_second), jnp.where(second, exit_first, exit_adjoint)], -1
    )
    back = lax.ppermute(other, axis, [(i, i ^ 1) for i in range(count)])
    both = jnp.where(second, jnp.concatenate([back, mine], 0), jnp.concatenate([mine, back], 0))
    return both[..., :width], both[..., width:]


def head_ring(part, count, axis):
    return [part] + [
        lax.ppermute(part, axis, [(i, (i + k) % count) for i in range(count)])
        for k in range(1, count)
    ]


def make_body(seq_count, head_devices):
    def body(queries, raw_keys, values, write_rate, out_weight, out_grad):
        head_count = write_rate.shape[1]
        head_width = queries.shape[1] // head_count
        token_count = queries.shape[0]
        width = queries.shape[1]
        here = lax.axis_index("head")

        rows = out_grad.shape[0]
        weight_cols = [lax.dynamic_slice_in_dim(out_weight, here * width, width, 1)]
        grad_parts = [out_grad]
        for k in range(1, head_devices):
            block = lax.dynamic_slice_in_dim(
                out_weight, ((here + k) % head_devices) * width, width, 1
            )
            moved = lax.ppermute(
                jnp.concatenate([out_grad, block], 0),
                "head",
                [(i, (i + k) % head_devices) for i in range(head_devices)],
            )
            grad_parts.append(moved[:rows])
            weight_cols.append(moved[rows:])
        weight_mine = jnp.concatenate(weight_cols, 0)

        weight_rows = jnp.concatenate(
            [
                lax.dynamic_slice_in_dim(
                    out_weight, ((here - k) % head_devices) * width, width, 1
                )
                for k in range(head_devices)
            ],
            1,
        )

        def factor_inputs(float_query, float_key, float_value, rates):
            return block_factors(
                to_blocks(float_query, head_count),
                to_blocks(float_key, head_count),
                to_blocks(float_value, head_count),
                rate_blocks(rates),
            )

        factors, pull_factors = jax.vjp(
            factor_inputs,
            queries.astype(jnp.float32),
            raw_keys.astype(jnp.float32),
            values.astype(jnp.float32),
            write_rate,
        )
        unit_query, unit_key, key_mix, value_mix, causal_scores = factors
        identity_heads = jnp.broadcast_to(
            jnp.eye(head_width, dtype=jnp.float32), (head_count, head_width, head_width)
        )
        zero_heads = jnp.zeros((head_count, head_width, head_width), jnp.float32)
        widened = (
            unit_query,
            unit_key,
            key_mix,
            jnp.concatenate([jnp.zeros_like(value_mix), value_mix], -1),
            causal_scores,
        )
        joined_state, joined_outputs = run_blocks(
            widened, jnp.concatenate([identity_heads, zero_heads], -1)
        )
        transition = joined_state[..., :head_width]
        offset = joined_state[..., head_width:]
        query_effect = joined_outputs[..., :head_width]
        attended_grad = lax.dot_general(
            jnp.concatenate(grad_parts, 1),
            weight_rows,
            (((1,), (1,)), ((), ())),
            preferred_element_type=jnp.float32,
        )
        grad_blocks = attended_grad.reshape(
            token_count // BLOCK, BLOCK, head_count, head_width
        ).transpose(0, 2, 1, 3)
        local_adjoint = jnp.einsum("nhcd,nhce->hde", query_effect, grad_blocks, precision=highest)
        entry_state, exit_adjoint = scan_both(transition, offset, local_adjoint, seq_count, "seq")

        def run_from_entry(factor_tuple):
            return run_blocks(factor_tuple, entry_state)

        (final_state, block_outputs), pull_run = jax.vjp(run_from_entry, factors)
        attended_bf = from_blocks(block_outputs).astype(jnp.bfloat16)
        attended_parts = head_ring(attended_bf, head_devices, "head")
        layer_out = jnp.dot(
            jnp.concatenate(attended_parts, 1), weight_mine, preferred_element_type=jnp.float32
        ).astype(jnp.bfloat16)
        factor_grads = pull_run((exit_adjoint, grad_blocks))
        query_part, key_part, value_part, rate_grad = pull_factors(factor_grads[0])
        return (
            layer_out,
            query_part.astype(jnp.bfloat16),
            key_part.astype(jnp.bfloat16),
            value_part.astype(jnp.bfloat16),
            rate_grad,
        )

    return body


def solution(mesh):
    placed = (
        P("seq", "head"),
        P("seq", "head"),
        P("seq", "head"),
        P("seq", "head"),
        P("head", None),
        P("seq", "head"),
    )
    return jax.shard_map(
        make_body(mesh.shape["seq"], mesh.shape["head"]),
        mesh=mesh,
        in_specs=placed,
        out_specs=(
            P("seq", "head"),
            P("seq", "head"),
            P("seq", "head"),
            P("seq", "head"),
            P("seq", "head"),
        ),
        check_vma=False,
    )
```

```python
import jax
import jax.numpy as jnp
from jax import lax
from jax.sharding import PartitionSpec as P

BLOCK = 64


epsilon = 1e-06
highest = lax.Precision.HIGHEST


def unit_rows(array):
    return array * lax.rsqrt(jnp.sum(array * array, -1, keepdims=True) + epsilon)


def to_blocks(array, head_count):
    rows = array.shape[0]
    head_width = array.shape[1] // head_count
    return array.reshape(rows // BLOCK, BLOCK, head_count, head_width).transpose(2, 0, 1, 3)


def rate_blocks(decay_rate):
    rows = decay_rate.shape[0]
    head_count = decay_rate.shape[1]
    return decay_rate.reshape(rows // BLOCK, BLOCK, head_count).transpose(2, 0, 1)


def from_blocks(block_outputs):
    block_count, head_count, size, head_width = block_outputs.shape
    return block_outputs.transpose(0, 2, 1, 3).reshape(block_count * size, head_count * head_width)


@jax.custom_vjp
def unit_lower_inverse(strict_lower):
    return unit_lower_inverse_fwd(strict_lower)[0]


def unit_lower_inverse_fwd(strict_lower):
    size = strict_lower.shape[-1]
    result = jnp.eye(size, dtype=jnp.float32) - strict_lower
    power_term = jnp.einsum("hnij,hnjk->hnik", strict_lower, strict_lower, precision=highest)
    span_done = 2
    while span_done < size:
        both = jnp.einsum(
            "hnij,hnjk->hnik",
            jnp.concatenate([power_term, result], -2),
            power_term,
            precision=highest,
        )
        power_term = both[..., :size, :]
        result = result + both[..., size:, :]
        span_done = span_done * 2
    return result, result


def unit_lower_inverse_bwd(result, grad):
    inner = jnp.einsum("hnji,hnjk->hnik", result, grad, precision=highest)
    outer = jnp.einsum("hnij,hnkj->hnik", inner, result, precision=highest)
    return (jnp.tril(-outer, -1),)


unit_lower_inverse.defvjp(unit_lower_inverse_fwd, unit_lower_inverse_bwd)


def block_factors(query_blocks, key_blocks, value_blocks, rate_parts):
    unit_query = unit_rows(query_blocks)
    unit_key = unit_rows(key_blocks)
    key_gram = jnp.einsum(
        "hncd,hnsd->hncs", unit_key * rate_parts[..., None], unit_key, precision=highest
    )
    strict_lower = jnp.tril(key_gram, -1)
    result = unit_lower_inverse(strict_lower)
    scaled = result * rate_parts[..., None, :]
    key_mix = jnp.einsum("hncs,hnsd->hncd", scaled, unit_key, precision=highest)
    value_mix = jnp.einsum("hncs,hnsd->hncd", scaled, value_blocks, precision=highest)
    causal_scores = jnp.tril(jnp.einsum("hncd,hnsd->hncs", unit_query, unit_key, precision=highest))
    return (unit_query, unit_key, key_mix, value_mix, causal_scores)


def run_blocks(factors, start_state):
    moved = tuple((jnp.moveaxis(member, 1, 0) for member in factors))

    def advance_block(state, pieces):
        unit_query, unit_key, key_mix, value_mix, causal_scores = pieces
        innovation = value_mix - jnp.einsum("hcd,hde->hce", key_mix, state, precision=highest)
        block_out = jnp.einsum("hcd,hde->hce", unit_query, state, precision=highest)
        block_out = block_out + jnp.einsum(
            "hcs,hse->hce", causal_scores, innovation, precision=highest
        )
        state = state + jnp.einsum("hcd,hce->hde", unit_key, innovation, precision=highest)
        return (state, block_out)

    return lax.scan(advance_block, start_state, moved, unroll=True)


def mm(left, right):
    return jnp.einsum("hij,hjk->hik", left, right, precision=highest)


def mm_t(left, right):
    return jnp.einsum("hji,hjk->hik", left, right, precision=highest)


def pick_head(array, index):
    return lax.dynamic_slice_in_dim(array, index, 1, 0)


def scan_both(transition, offset, local_adjoint, count, axis):
    place = lax.axis_index(axis)
    width = transition.shape[-1]
    core = place % 2
    own = jnp.concatenate([transition, offset, local_adjoint], -1)
    got = lax.ppermute(pick_head(own, 1 - core), axis, [(i, i ^ 1) for i in range(count)])
    mine = pick_head(own, core)
    second = core == 1
    low = jnp.where(second, got, mine)
    high = jnp.where(second, mine, got)
    core_low, core_high = low, high
    joined = mm(high[..., :width], jnp.concatenate([low[..., :width], low[..., width : 2 * width]], -1))
    total_map = joined[..., :width]
    total_shift = joined[..., width:] + high[..., width : 2 * width]
    total_adjoint = mm_t(low[..., :width], high[..., 2 * width :]) + low[..., 2 * width :]
    entry_map = entry_state = exit_map = exit_adjoint = None
    step = 2
    while step < count:
        last = 2 * step >= count
        pairs = [(i, i ^ step) for i in range(count)]
        upper = (place & step) != 0
        if last:
            sent = jnp.concatenate([total_shift, total_adjoint], -1)
        else:
            sent = jnp.concatenate([total_map, total_shift, total_adjoint], -1)
        got = lax.ppermute(sent, axis, pairs)
        low = jnp.where(upper, got, sent)
        high = jnp.where(upper, sent, got)
        if last:
            low_shift = low[..., :width]
            high_adjoint = high[..., width:]
        else:
            low_map, low_shift = low[..., :width], low[..., width : 2 * width]
            high_map, high_adjoint = high[..., :width], high[..., 2 * width :]
        if entry_map is None:
            entry_state = jnp.where(upper, low_shift, jnp.zeros_like(low_shift))
            exit_adjoint = jnp.where(upper, jnp.zeros_like(high_adjoint), high_adjoint)
            if not last:
                eye = jnp.broadcast_to(jnp.eye(width, dtype=jnp.float32), low_map.shape)
                entry_map = jnp.where(upper, low_map, eye)
                exit_map = jnp.where(upper, eye, jnp.swapaxes(high_map, 1, 2))
        else:
            entry_state = jnp.where(upper, entry_state + mm(entry_map, low_shift), entry_state)
            exit_adjoint = jnp.where(upper, exit_adjoint, exit_adjoint + mm(exit_map, high_adjoint))
            if not last:
                entry_map = jnp.where(upper, mm(entry_map, low_map), entry_map)
                exit_map = jnp.where(
                    upper, exit_map, jnp.einsum("hij,hkj->hik", exit_map, high_map, precision=highest)
                )
        if not last:
            joined = mm(high_map, jnp.concatenate([low_map, low_shift], -1))
            total_map = joined[..., :width]
            total_shift = joined[..., width:] + high[..., width : 2 * width]
            total_adjoint = mm_t(low_map, high_adjoint) + low[..., 2 * width :]
        step *= 2
    if entry_state is None:
        entry_state = jnp.zeros_like(total_shift)
        exit_adjoint = jnp.zeros_like(total_adjoint)
    entry_second = mm(core_low[..., :width], entry_state) + core_low[..., width : 2 * width]
    exit_first = mm_t(core_high[..., :width], exit_adjoint) + core_high[..., 2 * width :]
    mine = jnp.concatenate(
        [jnp.where(second, entry_second, entry_state), jnp.where(second, exit_adjoint, exit_first)], -1
    )
    other = jnp.concatenate(
        [jnp.where(second, entry_state, entry_second), jnp.where(second, exit_first, exit_adjoint)], -1
    )
    back = lax.ppermute(other, axis, [(i, i ^ 1) for i in range(count)])
    both = jnp.where(second, jnp.concatenate([back, mine], 0), jnp.concatenate([mine, back], 0))
    return both[..., :width], both[..., width:]


def head_ring(part, count, axis):
    return [part] + [
        lax.ppermute(part, axis, [(i, (i + k) % count) for i in range(count)])
        for k in range(1, count)
    ]


def make_body(seq_count, head_devices):
    def body(queries, raw_keys, values, write_rate, out_weight, out_grad):
        head_count = write_rate.shape[1]
        head_width = queries.shape[1] // head_count
        token_count = queries.shape[0]
        width = queries.shape[1]
        here = lax.axis_index("head")

        rows = out_grad.shape[0]
        weight_cols = [lax.dynamic_slice_in_dim(out_weight, here * width, width, 1)]
        grad_parts = [out_grad]
        for k in range(1, head_devices):
            block = lax.dynamic_slice_in_dim(
                out_weight, ((here + k) % head_devices) * width, width, 1
            )
            pairs = [(i, (i + k) % head_devices) for i in range(head_devices)]
            if block.shape[0] % rows == 0:
                moved = lax.ppermute(
                    jnp.concatenate([out_grad[None], block.reshape(-1, rows, width)], 0), "head", pairs
                )
                grad_parts.append(moved[0])
                weight_cols.append(moved[1:].reshape(-1, width))
            else:
                moved = lax.ppermute(jnp.concatenate([out_grad, block], 0), "head", pairs)
                grad_parts.append(moved[:rows])
                weight_cols.append(moved[rows:])
        weight_mine = jnp.concatenate(weight_cols, 0)

        weight_rows = jnp.concatenate(
            [
                lax.dynamic_slice_in_dim(
                    out_weight, ((here - k) % head_devices) * width, width, 1
                )
                for k in range(head_devices)
            ],
            1,
        )

        def factor_inputs(float_query, float_key, float_value, rates):
            return block_factors(
                to_blocks(float_query, head_count),
                to_blocks(float_key, head_count),
                to_blocks(float_value, head_count),
                rate_blocks(rates),
            )

        factors, pull_factors = jax.vjp(
            factor_inputs,
            queries.astype(jnp.float32),
            raw_keys.astype(jnp.float32),
            values.astype(jnp.float32),
            write_rate,
        )
        unit_query, unit_key, key_mix, value_mix, causal_scores = factors
        identity_heads = jnp.broadcast_to(
            jnp.eye(head_width, dtype=jnp.float32), (head_count, head_width, head_width)
        )
        zero_heads = jnp.zeros((head_count, head_width, head_width), jnp.float32)
        widened = (
            unit_query,
            unit_key,
            key_mix,
            jnp.concatenate([jnp.zeros_like(value_mix), value_mix], -1),
            causal_scores,
        )
        joined_state, joined_outputs = run_blocks(
            widened, jnp.concatenate([identity_heads, zero_heads], -1)
        )
        transition = joined_state[..., :head_width]
        offset = joined_state[..., head_width:]
        query_effect = joined_outputs[..., :head_width]
        attended_grad = lax.dot_general(
            jnp.concatenate(grad_parts, 1),
            weight_rows,
            (((1,), (1,)), ((), ())),
            preferred_element_type=jnp.float32,
        )
        grad_blocks = attended_grad.reshape(
            token_count // BLOCK, BLOCK, head_count, head_width
        ).transpose(0, 2, 1, 3)
        local_adjoint = jnp.einsum("nhcd,nhce->hde", query_effect, grad_blocks, precision=highest)
        entry_state, exit_adjoint = scan_both(transition, offset, local_adjoint, seq_count, "seq")

        def run_from_entry(factor_tuple):
            return run_blocks(factor_tuple, entry_state)

        (final_state, block_outputs), pull_run = jax.vjp(run_from_entry, factors)
        attended_bf = from_blocks(block_outputs).astype(jnp.bfloat16)
        attended_parts = head_ring(attended_bf, head_devices, "head")
        layer_out = jnp.dot(
            jnp.concatenate(attended_parts, 1), weight_mine, preferred_element_type=jnp.float32
        ).astype(jnp.bfloat16)
        factor_grads = pull_run((exit_adjoint, grad_blocks))
        query_part, key_part, value_part, rate_grad = pull_factors(factor_grads[0])
        return (
            layer_out,
            query_part.astype(jnp.bfloat16),
            key_part.astype(jnp.bfloat16),
            value_part.astype(jnp.bfloat16),
            rate_grad,
        )

    return body


def solution(mesh):
    placed = (
        P("seq", "head"),
        P("seq", "head"),
        P("seq", "head"),
        P("seq", "head"),
        P("head", None),
        P("seq", "head"),
    )
    return jax.shard_map(
        make_body(mesh.shape["seq"], mesh.shape["head"]),
        mesh=mesh,
        in_specs=placed,
        out_specs=(
            P("seq", "head"),
            P("seq", "head"),
            P("seq", "head"),
            P("seq", "head"),
            P("seq", "head"),
        ),
        check_vma=False,
    )
```

```python
import jax
import jax.numpy as jnp
from jax import lax
from jax.sharding import PartitionSpec as P

BLOCK = 64


epsilon = 1e-06
highest = lax.Precision.HIGHEST


def unit_rows(array):
    return array * lax.rsqrt(jnp.sum(array * array, -1, keepdims=True) + epsilon)


def to_blocks(array, head_count):
    rows = array.shape[0]
    head_width = array.shape[1] // head_count
    return array.reshape(rows // BLOCK, BLOCK, head_count, head_width).transpose(2, 0, 1, 3)


def rate_blocks(decay_rate):
    rows = decay_rate.shape[0]
    head_count = decay_rate.shape[1]
    return decay_rate.reshape(rows // BLOCK, BLOCK, head_count).transpose(2, 0, 1)


def from_blocks(block_outputs):
    block_count, head_count, size, head_width = block_outputs.shape
    return block_outputs.transpose(0, 2, 1, 3).reshape(block_count * size, head_count * head_width)


@jax.custom_vjp
def unit_lower_inverse(strict_lower):
    return unit_lower_inverse_fwd(strict_lower)[0]


def unit_lower_inverse_fwd(strict_lower):
    size = strict_lower.shape[-1]
    result = jnp.eye(size, dtype=jnp.float32) - strict_lower
    power_term = jnp.einsum("hnij,hnjk->hnik", strict_lower, strict_lower, precision=highest)
    span_done = 2
    while span_done < size:
        both = jnp.einsum(
            "hnij,hnjk->hnik",
            jnp.concatenate([power_term, result], -2),
            power_term,
            precision=highest,
        )
        power_term = both[..., :size, :]
        result = result + both[..., size:, :]
        span_done = span_done * 2
    return result, result


def unit_lower_inverse_bwd(result, grad):
    inner = jnp.einsum("hnji,hnjk->hnik", result, grad, precision=highest)
    outer = jnp.einsum("hnij,hnkj->hnik", inner, result, precision=highest)
    return (jnp.tril(-outer, -1),)


unit_lower_inverse.defvjp(unit_lower_inverse_fwd, unit_lower_inverse_bwd)


def block_factors(query_blocks, key_blocks, value_blocks, rate_parts):
    unit_query = unit_rows(query_blocks)
    unit_key = unit_rows(key_blocks)
    key_gram = jnp.einsum(
        "hncd,hnsd->hncs", unit_key * rate_parts[..., None], unit_key, precision=highest
    )
    strict_lower = jnp.tril(key_gram, -1)
    result = unit_lower_inverse(strict_lower)
    scaled = result * rate_parts[..., None, :]
    key_mix = jnp.einsum("hncs,hnsd->hncd", scaled, unit_key, precision=highest)
    value_mix = jnp.einsum("hncs,hnsd->hncd", scaled, value_blocks, precision=highest)
    causal_scores = jnp.tril(jnp.einsum("hncd,hnsd->hncs", unit_query, unit_key, precision=highest))
    return (unit_query, unit_key, key_mix, value_mix, causal_scores)


def run_blocks(factors, start_state):
    moved = tuple((jnp.moveaxis(member, 1, 0) for member in factors))

    def advance_block(state, pieces):
        unit_query, unit_key, key_mix, value_mix, causal_scores = pieces
        innovation = value_mix - jnp.einsum("hcd,hde->hce", key_mix, state, precision=highest)
        block_out = jnp.einsum("hcd,hde->hce", unit_query, state, precision=highest)
        block_out = block_out + jnp.einsum(
            "hcs,hse->hce", causal_scores, innovation, precision=highest
        )
        state = state + jnp.einsum("hcd,hce->hde", unit_key, innovation, precision=highest)
        return (state, block_out)

    return lax.scan(advance_block, start_state, moved, unroll=True)


def mm(left, right):
    return jnp.einsum("hij,hjk->hik", left, right, precision=highest)


def mm_t(left, right):
    return jnp.einsum("hji,hjk->hik", left, right, precision=highest)


def pick_head(array, index):
    return lax.dynamic_slice_in_dim(array, index, 1, 0)


def scan_both(transition, offset, local_adjoint, count, axis):
    place = lax.axis_index(axis)
    width = transition.shape[-1]
    core = place % 2
    own = jnp.concatenate([transition, offset, local_adjoint], -1)
    got = lax.ppermute(pick_head(own, 1 - core), axis, [(i, i ^ 1) for i in range(count)])
    mine = pick_head(own, core)
    second = core == 1
    low = jnp.where(second, got, mine)
    high = jnp.where(second, mine, got)
    core_low, core_high = low, high
    joined = mm(high[..., :width], jnp.concatenate([low[..., :width], low[..., width : 2 * width]], -1))
    total_map = joined[..., :width]
    total_shift = joined[..., width:] + high[..., width : 2 * width]
    total_adjoint = mm_t(low[..., :width], high[..., 2 * width :]) + low[..., 2 * width :]
    entry_map = entry_state = exit_map = exit_adjoint = None
    step = 2
    while step < count:
        last = 2 * step >= count
        pairs = [(i, i ^ step) for i in range(count)]
        upper = (place & step) != 0
        if last:
            sent = jnp.concatenate([total_shift, total_adjoint], -1)
        else:
            sent = jnp.concatenate([total_map, total_shift, total_adjoint], -1)
        got = lax.ppermute(sent, axis, pairs)
        low = jnp.where(upper, got, sent)
        high = jnp.where(upper, sent, got)
        if last:
            low_shift = low[..., :width]
            high_adjoint = high[..., width:]
        else:
            low_map, low_shift = low[..., :width], low[..., width : 2 * width]
            high_map, high_adjoint = high[..., :width], high[..., 2 * width :]
        if entry_map is None:
            entry_state = jnp.where(upper, low_shift, jnp.zeros_like(low_shift))
            exit_adjoint = jnp.where(upper, jnp.zeros_like(high_adjoint), high_adjoint)
            if not last:
                eye = jnp.broadcast_to(jnp.eye(width, dtype=jnp.float32), low_map.shape)
                entry_map = jnp.where(upper, low_map, eye)
                exit_map = jnp.where(upper, eye, jnp.swapaxes(high_map, 1, 2))
        else:
            entry_state = jnp.where(upper, entry_state + mm(entry_map, low_shift), entry_state)
            exit_adjoint = jnp.where(upper, exit_adjoint, exit_adjoint + mm(exit_map, high_adjoint))
            if not last:
                entry_map = jnp.where(upper, mm(entry_map, low_map), entry_map)
                exit_map = jnp.where(
                    upper, exit_map, jnp.einsum("hij,hkj->hik", exit_map, high_map, precision=highest)
                )
        if not last:
            joined = mm(high_map, jnp.concatenate([low_map, low_shift], -1))
            total_map = joined[..., :width]
            total_shift = joined[..., width:] + high[..., width : 2 * width]
            total_adjoint = mm_t(low_map, high_adjoint) + low[..., 2 * width :]
        step *= 2
    if entry_state is None:
        entry_state = jnp.zeros_like(total_shift)
        exit_adjoint = jnp.zeros_like(total_adjoint)
    entry_second = mm(core_low[..., :width], entry_state) + core_low[..., width : 2 * width]
    exit_first = mm_t(core_high[..., :width], exit_adjoint) + core_high[..., 2 * width :]
    mine = jnp.concatenate(
        [jnp.where(second, entry_second, entry_state), jnp.where(second, exit_adjoint, exit_first)], -1
    )
    other = jnp.concatenate(
        [jnp.where(second, entry_state, entry_second), jnp.where(second, exit_first, exit_adjoint)], -1
    )
    back = lax.ppermute(other, axis, [(i, i ^ 1) for i in range(count)])
    both = jnp.where(second, jnp.concatenate([back, mine], 0), jnp.concatenate([mine, back], 0))
    return both[..., :width], both[..., width:]


def head_ring(part, count, axis):
    return [part] + [
        lax.ppermute(part, axis, [(i, (i + k) % count) for i in range(count)])
        for k in range(1, count)
    ]


def make_body(seq_count, head_devices):
    def body(queries, raw_keys, values, write_rate, out_weight, out_grad):
        head_count = write_rate.shape[1]
        head_width = queries.shape[1] // head_count
        token_count = queries.shape[0]
        width = queries.shape[1]
        here = lax.axis_index("head")

        rows = out_grad.shape[0]
        grad_parts = head_ring(out_grad, head_devices, "head")

        weight_rows = jnp.concatenate(
            [
                lax.dynamic_slice_in_dim(
                    out_weight, ((here - k) % head_devices) * width, width, 1
                )
                for k in range(head_devices)
            ],
            1,
        )

        def factor_inputs(float_query, float_key, float_value, rates):
            return block_factors(
                to_blocks(float_query, head_count),
                to_blocks(float_key, head_count),
                to_blocks(float_value, head_count),
                rate_blocks(rates),
            )

        factors, pull_factors = jax.vjp(
            factor_inputs,
            queries.astype(jnp.float32),
            raw_keys.astype(jnp.float32),
            values.astype(jnp.float32),
            write_rate,
        )
        unit_query, unit_key, key_mix, value_mix, causal_scores = factors
        identity_heads = jnp.broadcast_to(
            jnp.eye(head_width, dtype=jnp.float32), (head_count, head_width, head_width)
        )
        zero_heads = jnp.zeros((head_count, head_width, head_width), jnp.float32)
        widened = (
            unit_query,
            unit_key,
            key_mix,
            jnp.concatenate([jnp.zeros_like(value_mix), value_mix], -1),
            causal_scores,
        )
        joined_state, joined_outputs = run_blocks(
            widened, jnp.concatenate([identity_heads, zero_heads], -1)
        )
        transition = joined_state[..., :head_width]
        offset = joined_state[..., head_width:]
        query_effect = joined_outputs[..., :head_width]
        attended_grad = lax.dot_general(
            jnp.concatenate(grad_parts, 1),
            weight_rows,
            (((1,), (1,)), ((), ())),
            preferred_element_type=jnp.float32,
        )
        grad_blocks = attended_grad.reshape(
            token_count // BLOCK, BLOCK, head_count, head_width
        ).transpose(0, 2, 1, 3)
        local_adjoint = jnp.einsum("nhcd,nhce->hde", query_effect, grad_blocks, precision=highest)
        entry_state, exit_adjoint = scan_both(transition, offset, local_adjoint, seq_count, "seq")

        def run_from_entry(factor_tuple):
            return run_blocks(factor_tuple, entry_state)

        (final_state, block_outputs), pull_run = jax.vjp(run_from_entry, factors)
        zero_outputs = joined_outputs[..., head_width:]
        attended = zero_outputs + jnp.einsum(
            "nhcd,hde->nhce", query_effect, entry_state, precision=highest
        )
        attended_bf = from_blocks(attended).astype(jnp.bfloat16)
        attended_parts = [attended_bf]
        weight_cols = [lax.dynamic_slice_in_dim(out_weight, here * width, width, 1)]
        for k in range(1, head_devices):
            block = lax.dynamic_slice_in_dim(
                out_weight, ((here + k) % head_devices) * width, width, 1
            )
            pairs = [(i, (i + k) % head_devices) for i in range(head_devices)]
            if block.shape[0] % rows == 0:
                moved = lax.ppermute(
                    jnp.concatenate([attended_bf[None], block.reshape(-1, rows, width)], 0),
                    "head",
                    pairs,
                )
                attended_parts.append(moved[0])
                weight_cols.append(moved[1:].reshape(-1, width))
            else:
                moved = lax.ppermute(jnp.concatenate([attended_bf, block], 0), "head", pairs)
                attended_parts.append(moved[:rows])
                weight_cols.append(moved[rows:])
        layer_out = jnp.dot(
            jnp.concatenate(attended_parts, 1),
            jnp.concatenate(weight_cols, 0),
            preferred_element_type=jnp.float32,
        ).astype(jnp.bfloat16)
        factor_grads = pull_run((exit_adjoint, grad_blocks))
        query_part, key_part, value_part, rate_grad = pull_factors(factor_grads[0])
        return (
            layer_out,
            query_part.astype(jnp.bfloat16),
            key_part.astype(jnp.bfloat16),
            value_part.astype(jnp.bfloat16),
            rate_grad,
        )

    return body


def solution(mesh):
    placed = (
        P("seq", "head"),
        P("seq", "head"),
        P("seq", "head"),
        P("seq", "head"),
        P("head", None),
        P("seq", "head"),
    )
    return jax.shard_map(
        make_body(mesh.shape["seq"], mesh.shape["head"]),
        mesh=mesh,
        in_specs=placed,
        out_specs=(
            P("seq", "head"),
            P("seq", "head"),
            P("seq", "head"),
            P("seq", "head"),
            P("seq", "head"),
        ),
        check_vma=False,
    )
```

```python
import jax
import jax.numpy as jnp
from jax import lax
from jax.sharding import PartitionSpec as P


BLOCK = 64


epsilon = 1e-06
highest = lax.Precision.HIGHEST


def unit_rows(array):
    return array * lax.rsqrt(jnp.sum(array * array, -1, keepdims=True) + epsilon)


def to_blocks(array, head_count):
    rows = array.shape[0]
    head_width = array.shape[1] // head_count
    return array.reshape(rows // BLOCK, BLOCK, head_count, head_width).transpose(2, 0, 1, 3)


def rate_blocks(decay_rate):
    rows = decay_rate.shape[0]
    head_count = decay_rate.shape[1]
    return decay_rate.reshape(rows // BLOCK, BLOCK, head_count).transpose(2, 0, 1)


def from_blocks(block_outputs):
    block_count, head_count, size, head_width = block_outputs.shape
    return block_outputs.transpose(0, 2, 1, 3).reshape(block_count * size, head_count * head_width)


@jax.custom_vjp
def unit_lower_inverse(strict_lower):
    return unit_lower_inverse_fwd(strict_lower)[0]


def unit_lower_inverse_fwd(strict_lower):
    size = strict_lower.shape[-1]
    result = jnp.eye(size, dtype=jnp.float32) - strict_lower
    power_term = jnp.einsum("hnij,hnjk->hnik", strict_lower, strict_lower, precision=highest)
    span_done = 2
    while span_done < size:
        both = jnp.einsum(
            "hnij,hnjk->hnik",
            jnp.concatenate([power_term, result], -2),
            power_term,
            precision=highest,
        )
        power_term = both[..., :size, :]
        result = result + both[..., size:, :]
        span_done = span_done * 2
    return result, result


def unit_lower_inverse_bwd(result, grad):
    inner = jnp.einsum("hnji,hnjk->hnik", result, grad, precision=highest)
    outer = jnp.einsum("hnij,hnkj->hnik", inner, result, precision=highest)
    return (jnp.tril(-outer, -1),)


unit_lower_inverse.defvjp(unit_lower_inverse_fwd, unit_lower_inverse_bwd)


def block_factors(query_blocks, key_blocks, value_blocks, rate_parts):
    unit_query = unit_rows(query_blocks)
    unit_key = unit_rows(key_blocks)
    key_gram = jnp.einsum(
        "hncd,hnsd->hncs", unit_key * rate_parts[..., None], unit_key, precision=highest
    )
    strict_lower = jnp.tril(key_gram, -1)
    result = unit_lower_inverse(strict_lower)
    scaled = result * rate_parts[..., None, :]
    key_mix = jnp.einsum("hncs,hnsd->hncd", scaled, unit_key, precision=highest)
    value_mix = jnp.einsum("hncs,hnsd->hncd", scaled, value_blocks, precision=highest)
    causal_scores = jnp.tril(jnp.einsum("hncd,hnsd->hncs", unit_query, unit_key, precision=highest))
    return (unit_query, unit_key, key_mix, value_mix, causal_scores)


def run_blocks(factors, start_state):
    moved = tuple((jnp.moveaxis(member, 1, 0) for member in factors))

    def advance_block(state, pieces):
        unit_query, unit_key, key_mix, value_mix, causal_scores = pieces
        innovation = value_mix - jnp.einsum("hcd,hde->hce", key_mix, state, precision=highest)
        block_out = jnp.einsum("hcd,hde->hce", unit_query, state, precision=highest)
        block_out = block_out + jnp.einsum(
            "hcs,hse->hce", causal_scores, innovation, precision=highest
        )
        state = state + jnp.einsum("hcd,hce->hde", unit_key, innovation, precision=highest)
        return (state, block_out)

    return lax.scan(advance_block, start_state, moved, unroll=True)


def mm(left, right):
    return jnp.einsum("hij,hjk->hik", left, right, precision=highest)


def mm_t(left, right):
    return jnp.einsum("hji,hjk->hik", left, right, precision=highest)


def pick_head(array, index):
    return lax.dynamic_slice_in_dim(array, index, 1, 0)


def scan_both(transition, offset, local_adjoint, count, axis):
    place = lax.axis_index(axis)
    width = transition.shape[-1]
    core = place % 2
    own = jnp.concatenate([transition, offset, local_adjoint], -1)
    got = lax.ppermute(pick_head(own, 1 - core), axis, [(i, i ^ 1) for i in range(count)])
    mine = pick_head(own, core)
    second = core == 1
    low = jnp.where(second, got, mine)
    high = jnp.where(second, mine, got)
    core_low, core_high = low, high
    joined = mm(high[..., :width], jnp.concatenate([low[..., :width], low[..., width : 2 * width]], -1))
    total_map = joined[..., :width]
    total_shift = joined[..., width:] + high[..., width : 2 * width]
    total_adjoint = mm_t(low[..., :width], high[..., 2 * width :]) + low[..., 2 * width :]
    entry_map = entry_state = exit_map = exit_adjoint = None
    step = 2
    while step < count:
        last = 2 * step >= count
        pairs = [(i, i ^ step) for i in range(count)]
        upper = (place & step) != 0
        if last:
            sent = jnp.concatenate([total_shift, total_adjoint], -1)
        else:
            sent = jnp.concatenate([total_map, total_shift, total_adjoint], -1)
        got = lax.ppermute(sent, axis, pairs)
        low = jnp.where(upper, got, sent)
        high = jnp.where(upper, sent, got)
        if last:
            low_shift = low[..., :width]
            high_adjoint = high[..., width:]
        else:
            low_map, low_shift = low[..., :width], low[..., width : 2 * width]
            high_map, high_adjoint = high[..., :width], high[..., 2 * width :]
        if entry_map is None:
            entry_state = jnp.where(upper, low_shift, jnp.zeros_like(low_shift))
            exit_adjoint = jnp.where(upper, jnp.zeros_like(high_adjoint), high_adjoint)
            if not last:
                eye = jnp.broadcast_to(jnp.eye(width, dtype=jnp.float32), low_map.shape)
                entry_map = jnp.where(upper, low_map, eye)
                exit_map = jnp.where(upper, eye, jnp.swapaxes(high_map, 1, 2))
        else:
            entry_state = jnp.where(upper, entry_state + mm(entry_map, low_shift), entry_state)
            exit_adjoint = jnp.where(upper, exit_adjoint, exit_adjoint + mm(exit_map, high_adjoint))
            if not last:
                entry_map = jnp.where(upper, mm(entry_map, low_map), entry_map)
                exit_map = jnp.where(
                    upper, exit_map, jnp.einsum("hij,hkj->hik", exit_map, high_map, precision=highest)
                )
        if not last:
            joined = mm(high_map, jnp.concatenate([low_map, low_shift], -1))
            total_map = joined[..., :width]
            total_shift = joined[..., width:] + high[..., width : 2 * width]
            total_adjoint = mm_t(low_map, high_adjoint) + low[..., 2 * width :]
        step *= 2
    if entry_state is None:
        entry_state = jnp.zeros_like(total_shift)
        exit_adjoint = jnp.zeros_like(total_adjoint)
    entry_second = mm(core_low[..., :width], entry_state) + core_low[..., width : 2 * width]
    exit_first = mm_t(core_high[..., :width], exit_adjoint) + core_high[..., 2 * width :]
    mine = jnp.concatenate(
        [jnp.where(second, entry_second, entry_state), jnp.where(second, exit_adjoint, exit_first)], -1
    )
    other = jnp.concatenate(
        [jnp.where(second, entry_state, entry_second), jnp.where(second, exit_first, exit_adjoint)], -1
    )
    back = lax.ppermute(other, axis, [(i, i ^ 1) for i in range(count)])
    both = jnp.where(second, jnp.concatenate([back, mine], 0), jnp.concatenate([mine, back], 0))
    return both[..., :width], both[..., width:]


def head_ring(part, count, axis):
    return [part] + [
        lax.ppermute(part, axis, [(i, (i + k) % count) for i in range(count)])
        for k in range(1, count)
    ]


def make_body(seq_count, head_devices):
    def body(queries, raw_keys, values, write_rate, out_weight, out_grad):
        head_count = write_rate.shape[1]
        head_width = queries.shape[1] // head_count
        token_count = queries.shape[0]
        width = queries.shape[1]
        here = lax.axis_index("head")

        weight_rows = jnp.concatenate(
            [
                lax.dynamic_slice_in_dim(
                    out_weight, ((here - k) % head_devices) * width, width, 1
                )
                for k in range(head_devices)
            ],
            1,
        )

        def factor_inputs(float_query, float_key, float_value, rates):
            return block_factors(
                to_blocks(float_query, head_count),
                to_blocks(float_key, head_count),
                to_blocks(float_value, head_count),
                rate_blocks(rates),
            )

        factors, pull_factors = jax.vjp(
            factor_inputs,
            queries.astype(jnp.float32),
            raw_keys.astype(jnp.float32),
            values.astype(jnp.float32),
            write_rate,
        )
        unit_query, unit_key, key_mix, value_mix, causal_scores = factors
        late_grad, _ = lax.optimization_barrier((out_grad, key_mix))
        grad_parts = head_ring(late_grad, head_devices, "head")
        identity_heads = jnp.broadcast_to(
            jnp.eye(head_width, dtype=jnp.float32), (head_count, head_width, head_width)
        )
        zero_heads = jnp.zeros((head_count, head_width, head_width), jnp.float32)
        widened = (
            unit_query,
            unit_key,
            key_mix,
            jnp.concatenate([jnp.zeros_like(value_mix), value_mix], -1),
            causal_scores,
        )
        joined_state, joined_outputs = run_blocks(
            widened, jnp.concatenate([identity_heads, zero_heads], -1)
        )
        transition = joined_state[..., :head_width]
        offset = joined_state[..., head_width:]
        query_effect = joined_outputs[..., :head_width]
        attended_grad = lax.dot_general(
            jnp.concatenate(grad_parts, 1),
            weight_rows,
            (((1,), (1,)), ((), ())),
            preferred_element_type=jnp.float32,
        )
        grad_blocks = attended_grad.reshape(
            token_count // BLOCK, BLOCK, head_count, head_width
        ).transpose(0, 2, 1, 3)
        local_adjoint = jnp.einsum("nhcd,nhce->hde", query_effect, grad_blocks, precision=highest)
        weight_cols = [lax.dynamic_slice_in_dim(out_weight, here * width, width, 1)]
        for k in range(1, head_devices):
            block = lax.dynamic_slice_in_dim(
                out_weight, ((here + k) % head_devices) * width, width, 1
            )
            weight_cols.append(
                lax.ppermute(
                    block, "head", [(i, (i + k) % head_devices) for i in range(head_devices)]
                )
            )
        weight_mine = jnp.concatenate(weight_cols, 0)
        entry_state, exit_adjoint = scan_both(transition, offset, local_adjoint, seq_count, "seq")

        def run_from_entry(factor_tuple):
            return run_blocks(factor_tuple, entry_state)

        (final_state, block_outputs), pull_run = jax.vjp(run_from_entry, factors)
        attended_bf = from_blocks(block_outputs).astype(jnp.bfloat16)
        attended_parts = head_ring(attended_bf, head_devices, "head")
        layer_out = jnp.dot(
            jnp.concatenate(attended_parts, 1), weight_mine, preferred_element_type=jnp.float32
        ).astype(jnp.bfloat16)
        factor_grads = pull_run((exit_adjoint, grad_blocks))
        query_part, key_part, value_part, rate_grad = pull_factors(factor_grads[0])
        return (
            layer_out,
            query_part.astype(jnp.bfloat16),
            key_part.astype(jnp.bfloat16),
            value_part.astype(jnp.bfloat16),
            rate_grad,
        )

    return body


def solution(mesh):
    placed = (
        P("seq", "head"),
        P("seq", "head"),
        P("seq", "head"),
        P("seq", "head"),
        P("head", None),
        P("seq", "head"),
    )
    return jax.shard_map(
        make_body(mesh.shape["seq"], mesh.shape["head"]),
        mesh=mesh,
        in_specs=placed,
        out_specs=(
            P("seq", "head"),
            P("seq", "head"),
            P("seq", "head"),
            P("seq", "head"),
            P("seq", "head"),
        ),
        check_vma=False,
    )
```

```python
import jax
import jax.numpy as jnp
from jax import lax
from jax.sharding import PartitionSpec as P


BLOCK = 64


epsilon = 1e-06
highest = lax.Precision.HIGHEST


def unit_rows(array):
    return array * lax.rsqrt(jnp.sum(array * array, -1, keepdims=True) + epsilon)


def to_blocks(array, head_count):
    rows = array.shape[0]
    head_width = array.shape[1] // head_count
    return array.reshape(rows // BLOCK, BLOCK, head_count, head_width)


def rate_blocks(decay_rate):
    rows = decay_rate.shape[0]
    head_count = decay_rate.shape[1]
    return decay_rate.reshape(rows // BLOCK, BLOCK, head_count)


def from_blocks(block_outputs):
    block_count, size, head_count, head_width = block_outputs.shape
    return block_outputs.reshape(block_count * size, head_count * head_width)


@jax.custom_vjp
def unit_lower_inverse(strict_lower):
    return unit_lower_inverse_fwd(strict_lower)[0]


def unit_lower_inverse_fwd(strict_lower):
    size = strict_lower.shape[-1]
    result = jnp.eye(size, dtype=jnp.float32) - strict_lower
    power_term = jnp.einsum("hnij,hnjk->hnik", strict_lower, strict_lower, precision=highest)
    span_done = 2
    while span_done < size:
        both = jnp.einsum(
            "hnij,hnjk->hnik",
            jnp.concatenate([power_term, result], -2),
            power_term,
            precision=highest,
        )
        power_term = both[..., :size, :]
        result = result + both[..., size:, :]
        span_done = span_done * 2
    return result, result


def unit_lower_inverse_bwd(result, grad):
    inner = jnp.einsum("hnji,hnjk->hnik", result, grad, precision=highest)
    outer = jnp.einsum("hnij,hnkj->hnik", inner, result, precision=highest)
    return (jnp.tril(-outer, -1),)


unit_lower_inverse.defvjp(unit_lower_inverse_fwd, unit_lower_inverse_bwd)


def block_factors(query_blocks, key_blocks, value_blocks, rate_parts):
    unit_query = unit_rows(query_blocks)
    unit_key = unit_rows(key_blocks)
    key_gram = jnp.einsum(
        "nchd,nshd->hncs", unit_key * rate_parts[..., None], unit_key, precision=highest
    )
    strict_lower = jnp.tril(key_gram, -1)
    result = unit_lower_inverse(strict_lower)
    scaled = result * jnp.transpose(rate_parts, (2, 0, 1))[..., None, :]
    key_mix = jnp.einsum("hncs,nshd->nchd", scaled, unit_key, precision=highest)
    value_mix = jnp.einsum("hncs,nshd->nchd", scaled, value_blocks, precision=highest)
    causal_scores = jnp.tril(jnp.einsum("nchd,nshd->hncs", unit_query, unit_key, precision=highest))
    return (unit_query, unit_key, key_mix, value_mix, causal_scores)


def run_blocks(factors, start_state):
    unit_query, unit_key, key_mix, value_mix, causal_scores = factors
    moved = (unit_query, unit_key, key_mix, value_mix, jnp.moveaxis(causal_scores, 1, 0))

    def advance_block(state, pieces):
        unit_query, unit_key, key_mix, value_mix, causal_scores = pieces
        innovation = value_mix - jnp.einsum("chd,hde->che", key_mix, state, precision=highest)
        block_out = jnp.einsum("chd,hde->che", unit_query, state, precision=highest)
        block_out = block_out + jnp.einsum(
            "hcs,she->che", causal_scores, innovation, precision=highest
        )
        state = state + jnp.einsum("chd,che->hde", unit_key, innovation, precision=highest)
        return (state, block_out)

    return lax.scan(advance_block, start_state, moved, unroll=True)


def mm(left, right):
    return jnp.einsum("hij,hjk->hik", left, right, precision=highest)


def mm_t(left, right):
    return jnp.einsum("hji,hjk->hik", left, right, precision=highest)


def pick_head(array, index):
    return lax.dynamic_slice_in_dim(array, index, 1, 0)


def scan_both(transition, offset, local_adjoint, count, axis):
    place = lax.axis_index(axis)
    width = transition.shape[-1]
    core = place % 2
    own = jnp.concatenate([transition, offset, local_adjoint], -1)
    got = lax.ppermute(pick_head(own, 1 - core), axis, [(i, i ^ 1) for i in range(count)])
    mine = pick_head(own, core)
    second = core == 1
    low = jnp.where(second, got, mine)
    high = jnp.where(second, mine, got)
    core_low, core_high = low, high
    joined = mm(high[..., :width], jnp.concatenate([low[..., :width], low[..., width : 2 * width]], -1))
    total_map = joined[..., :width]
    total_shift = joined[..., width:] + high[..., width : 2 * width]
    total_adjoint = mm_t(low[..., :width], high[..., 2 * width :]) + low[..., 2 * width :]
    entry_map = entry_state = exit_map = exit_adjoint = None
    step = 2
    while step < count:
        last = 2 * step >= count
        pairs = [(i, i ^ step) for i in range(count)]
        upper = (place & step) != 0
        if last:
            sent = jnp.concatenate([total_shift, total_adjoint], -1)
        else:
            sent = jnp.concatenate([total_map, total_shift, total_adjoint], -1)
        got = lax.ppermute(sent, axis, pairs)
        low = jnp.where(upper, got, sent)
        high = jnp.where(upper, sent, got)
        if last:
            low_shift = low[..., :width]
            high_adjoint = high[..., width:]
        else:
            low_map, low_shift = low[..., :width], low[..., width : 2 * width]
            high_map, high_adjoint = high[..., :width], high[..., 2 * width :]
        if entry_map is None:
            entry_state = jnp.where(upper, low_shift, jnp.zeros_like(low_shift))
            exit_adjoint = jnp.where(upper, jnp.zeros_like(high_adjoint), high_adjoint)
            if not last:
                eye = jnp.broadcast_to(jnp.eye(width, dtype=jnp.float32), low_map.shape)
                entry_map = jnp.where(upper, low_map, eye)
                exit_map = jnp.where(upper, eye, jnp.swapaxes(high_map, 1, 2))
        else:
            entry_state = jnp.where(upper, entry_state + mm(entry_map, low_shift), entry_state)
            exit_adjoint = jnp.where(upper, exit_adjoint, exit_adjoint + mm(exit_map, high_adjoint))
            if not last:
                entry_map = jnp.where(upper, mm(entry_map, low_map), entry_map)
                exit_map = jnp.where(
                    upper, exit_map, jnp.einsum("hij,hkj->hik", exit_map, high_map, precision=highest)
                )
        if not last:
            joined = mm(high_map, jnp.concatenate([low_map, low_shift], -1))
            total_map = joined[..., :width]
            total_shift = joined[..., width:] + high[..., width : 2 * width]
            total_adjoint = mm_t(low_map, high_adjoint) + low[..., 2 * width :]
        step *= 2
    if entry_state is None:
        entry_state = jnp.zeros_like(total_shift)
        exit_adjoint = jnp.zeros_like(total_adjoint)
    entry_second = mm(core_low[..., :width], entry_state) + core_low[..., width : 2 * width]
    exit_first = mm_t(core_high[..., :width], exit_adjoint) + core_high[..., 2 * width :]
    mine = jnp.concatenate(
        [jnp.where(second, entry_second, entry_state), jnp.where(second, exit_adjoint, exit_first)], -1
    )
    other = jnp.concatenate(
        [jnp.where(second, entry_state, entry_second), jnp.where(second, exit_first, exit_adjoint)], -1
    )
    back = lax.ppermute(other, axis, [(i, i ^ 1) for i in range(count)])
    both = jnp.where(second, jnp.concatenate([back, mine], 0), jnp.concatenate([mine, back], 0))
    return both[..., :width], both[..., width:]


def head_ring(part, count, axis):
    return [part] + [
        lax.ppermute(part, axis, [(i, (i + k) % count) for i in range(count)])
        for k in range(1, count)
    ]


def make_body(seq_count, head_devices):
    def body(queries, raw_keys, values, write_rate, out_weight, out_grad):
        head_count = write_rate.shape[1]
        head_width = queries.shape[1] // head_count
        token_count = queries.shape[0]
        width = queries.shape[1]
        here = lax.axis_index("head")

        grad_parts = head_ring(out_grad, head_devices, "head")

        weight_rows = jnp.concatenate(
            [
                lax.dynamic_slice_in_dim(
                    out_weight, ((here - k) % head_devices) * width, width, 1
                )
                for k in range(head_devices)
            ],
            1,
        )

        def factor_inputs(float_query, float_key, float_value, rates):
            return block_factors(
                to_blocks(float_query, head_count),
                to_blocks(float_key, head_count),
                to_blocks(float_value, head_count),
                rate_blocks(rates),
            )

        factors, pull_factors = jax.vjp(
            factor_inputs,
            queries.astype(jnp.float32),
            raw_keys.astype(jnp.float32),
            values.astype(jnp.float32),
            write_rate,
        )
        unit_query, unit_key, key_mix, value_mix, causal_scores = factors
        identity_heads = jnp.broadcast_to(
            jnp.eye(head_width, dtype=jnp.float32), (head_count, head_width, head_width)
        )
        zero_heads = jnp.zeros((head_count, head_width, head_width), jnp.float32)
        widened = (
            unit_query,
            unit_key,
            key_mix,
            jnp.concatenate([jnp.zeros_like(value_mix), value_mix], -1),
            causal_scores,
        )
        joined_state, joined_outputs = run_blocks(
            widened, jnp.concatenate([identity_heads, zero_heads], -1)
        )
        transition = joined_state[..., :head_width]
        offset = joined_state[..., head_width:]
        query_effect = joined_outputs[..., :head_width]
        attended_grad = lax.dot_general(
            jnp.concatenate(grad_parts, 1),
            weight_rows,
            (((1,), (1,)), ((), ())),
            preferred_element_type=jnp.float32,
        )
        grad_blocks = attended_grad.reshape(token_count // BLOCK, BLOCK, head_count, head_width)
        local_adjoint = jnp.einsum("nchd,nche->hde", query_effect, grad_blocks, precision=highest)
        weight_cols = [lax.dynamic_slice_in_dim(out_weight, here * width, width, 1)]
        for k in range(1, head_devices):
            block = lax.dynamic_slice_in_dim(
                out_weight, ((here + k) % head_devices) * width, width, 1
            )
            weight_cols.append(
                lax.ppermute(
                    block, "head", [(i, (i + k) % head_devices) for i in range(head_devices)]
                )
            )
        weight_mine = jnp.concatenate(weight_cols, 0)
        entry_state, exit_adjoint = scan_both(transition, offset, local_adjoint, seq_count, "seq")

        def run_from_entry(factor_tuple):
            return run_blocks(factor_tuple, entry_state)

        (final_state, block_outputs), pull_run = jax.vjp(run_from_entry, factors)
        attended_bf = from_blocks(block_outputs).astype(jnp.bfloat16)
        if head_devices == 4:
            first = lax.ppermute(attended_bf, "head", [(i, (i + 1) % 4) for i in range(4)])
            second = lax.ppermute(
                jnp.stack([attended_bf, first]), "head", [(i, (i + 2) % 4) for i in range(4)]
            )
            attended_parts = [attended_bf, first, second[0], second[1]]
        else:
            attended_parts = head_ring(attended_bf, head_devices, "head")
        layer_out = jnp.dot(
            jnp.concatenate(attended_parts, 1), weight_mine, preferred_element_type=jnp.float32
        ).astype(jnp.bfloat16)
        factor_grads = pull_run((exit_adjoint, grad_blocks))
        query_part, key_part, value_part, rate_grad = pull_factors(factor_grads[0])
        return (
            layer_out,
            query_part.astype(jnp.bfloat16),
            key_part.astype(jnp.bfloat16),
            value_part.astype(jnp.bfloat16),
            rate_grad,
        )

    return body


def solution(mesh):
    placed = (
        P("seq", "head"),
        P("seq", "head"),
        P("seq", "head"),
        P("seq", "head"),
        P("head", None),
        P("seq", "head"),
    )
    return jax.shard_map(
        make_body(mesh.shape["seq"], mesh.shape["head"]),
        mesh=mesh,
        in_specs=placed,
        out_specs=(
            P("seq", "head"),
            P("seq", "head"),
            P("seq", "head"),
            P("seq", "head"),
            P("seq", "head"),
        ),
        check_vma=False,
    )
```

```python
import jax
import jax.numpy as jnp
from jax import lax
from jax.sharding import PartitionSpec as P


BLOCK = 64


epsilon = 1e-06
highest = lax.Precision.HIGHEST


def unit_rows(array):
    return array * lax.rsqrt(jnp.sum(array * array, -1, keepdims=True) + epsilon)


def to_blocks(array, head_count):
    rows = array.shape[0]
    head_width = array.shape[1] // head_count
    return array.reshape(rows // BLOCK, BLOCK, head_count, head_width)


def rate_blocks(decay_rate):
    rows = decay_rate.shape[0]
    head_count = decay_rate.shape[1]
    return decay_rate.reshape(rows // BLOCK, BLOCK, head_count)


def from_blocks(block_outputs):
    block_count, size, head_count, head_width = block_outputs.shape
    return block_outputs.reshape(block_count * size, head_count * head_width)


@jax.custom_vjp
def unit_lower_inverse(strict_lower):
    return unit_lower_inverse_fwd(strict_lower)[0]


def unit_lower_inverse_fwd(strict_lower):
    size = strict_lower.shape[-1]
    result = jnp.eye(size, dtype=jnp.float32) - strict_lower
    power_term = jnp.einsum("hnij,hnjk->hnik", strict_lower, strict_lower, precision=highest)
    span_done = 2
    while span_done < size:
        both = jnp.einsum(
            "hnij,hnjk->hnik",
            jnp.concatenate([power_term, result], -2),
            power_term,
            precision=highest,
        )
        power_term = both[..., :size, :]
        result = result + both[..., size:, :]
        span_done = span_done * 2
    return result, result


def unit_lower_inverse_bwd(result, grad):
    inner = jnp.einsum("hnji,hnjk->hnik", result, grad, precision=highest)
    outer = jnp.einsum("hnij,hnkj->hnik", inner, result, precision=highest)
    return (jnp.tril(-outer, -1),)


unit_lower_inverse.defvjp(unit_lower_inverse_fwd, unit_lower_inverse_bwd)


def block_factors(query_blocks, key_blocks, value_blocks, rate_parts):
    unit_query = unit_rows(query_blocks)
    unit_key = unit_rows(key_blocks)
    key_gram = jnp.einsum(
        "nchd,nshd->hncs", unit_key * rate_parts[..., None], unit_key, precision=highest
    )
    strict_lower = jnp.tril(key_gram, -1)
    result = unit_lower_inverse(strict_lower)
    scaled = result * jnp.transpose(rate_parts, (2, 0, 1))[..., None, :]
    key_mix = jnp.einsum("hncs,nshd->nchd", scaled, unit_key, precision=highest)
    value_mix = jnp.einsum("hncs,nshd->nchd", scaled, value_blocks, precision=highest)
    causal_scores = jnp.tril(jnp.einsum("nchd,nshd->hncs", unit_query, unit_key, precision=highest))
    return (unit_query, unit_key, key_mix, value_mix, causal_scores)


def run_blocks(factors, start_state):
    unit_query, unit_key, key_mix, value_mix, causal_scores = factors
    moved = (unit_query, unit_key, key_mix, value_mix, jnp.moveaxis(causal_scores, 1, 0))

    def advance_block(state, pieces):
        unit_query, unit_key, key_mix, value_mix, causal_scores = pieces
        innovation = value_mix - jnp.einsum("chd,hde->che", key_mix, state, precision=highest)
        block_out = jnp.einsum("chd,hde->che", unit_query, state, precision=highest)
        block_out = block_out + jnp.einsum(
            "hcs,she->che", causal_scores, innovation, precision=highest
        )
        state = state + jnp.einsum("chd,che->hde", unit_key, innovation, precision=highest)
        return (state, block_out)

    return lax.scan(advance_block, start_state, moved, unroll=True)


def mm(left, right):
    return jnp.einsum("hij,hjk->hik", left, right, precision=highest)


def mm_t(left, right):
    return jnp.einsum("hji,hjk->hik", left, right, precision=highest)


def pick_head(array, index):
    return lax.dynamic_slice_in_dim(array, index, 1, 0)


def scan_both(transition, offset, local_adjoint, count, axis):
    place = lax.axis_index(axis)
    width = transition.shape[-1]
    core = place % 2
    own = jnp.concatenate([transition, offset, local_adjoint], -1)
    got = lax.ppermute(pick_head(own, 1 - core), axis, [(i, i ^ 1) for i in range(count)])
    mine = pick_head(own, core)
    second = core == 1
    low = jnp.where(second, got, mine)
    high = jnp.where(second, mine, got)
    core_low, core_high = low, high
    joined = mm(high[..., :width], jnp.concatenate([low[..., :width], low[..., width : 2 * width]], -1))
    total_map = joined[..., :width]
    total_shift = joined[..., width:] + high[..., width : 2 * width]
    total_adjoint = mm_t(low[..., :width], high[..., 2 * width :]) + low[..., 2 * width :]
    entry_map = entry_state = exit_map = exit_adjoint = None
    step = 2
    while step < count:
        last = 2 * step >= count
        pairs = [(i, i ^ step) for i in range(count)]
        upper = (place & step) != 0
        if last:
            sent = jnp.concatenate([total_shift, total_adjoint], -1)
        else:
            sent = jnp.concatenate([total_map, total_shift, total_adjoint], -1)
        got = lax.ppermute(sent, axis, pairs)
        low = jnp.where(upper, got, sent)
        high = jnp.where(upper, sent, got)
        if last:
            low_shift = low[..., :width]
            high_adjoint = high[..., width:]
        else:
            low_map, low_shift = low[..., :width], low[..., width : 2 * width]
            high_map, high_adjoint = high[..., :width], high[..., 2 * width :]
        if entry_map is None:
            entry_state = jnp.where(upper, low_shift, jnp.zeros_like(low_shift))
            exit_adjoint = jnp.where(upper, jnp.zeros_like(high_adjoint), high_adjoint)
            if not last:
                eye = jnp.broadcast_to(jnp.eye(width, dtype=jnp.float32), low_map.shape)
                entry_map = jnp.where(upper, low_map, eye)
                exit_map = jnp.where(upper, eye, jnp.swapaxes(high_map, 1, 2))
        else:
            entry_state = jnp.where(upper, entry_state + mm(entry_map, low_shift), entry_state)
            exit_adjoint = jnp.where(upper, exit_adjoint, exit_adjoint + mm(exit_map, high_adjoint))
            if not last:
                entry_map = jnp.where(upper, mm(entry_map, low_map), entry_map)
                exit_map = jnp.where(
                    upper, exit_map, jnp.einsum("hij,hkj->hik", exit_map, high_map, precision=highest)
                )
        if not last:
            joined = mm(high_map, jnp.concatenate([low_map, low_shift], -1))
            total_map = joined[..., :width]
            total_shift = joined[..., width:] + high[..., width : 2 * width]
            total_adjoint = mm_t(low_map, high_adjoint) + low[..., 2 * width :]
        step *= 2
    if entry_state is None:
        entry_state = jnp.zeros_like(total_shift)
        exit_adjoint = jnp.zeros_like(total_adjoint)
    entry_second = mm(core_low[..., :width], entry_state) + core_low[..., width : 2 * width]
    exit_first = mm_t(core_high[..., :width], exit_adjoint) + core_high[..., 2 * width :]
    mine = jnp.concatenate(
        [jnp.where(second, entry_second, entry_state), jnp.where(second, exit_adjoint, exit_first)], -1
    )
    other = jnp.concatenate(
        [jnp.where(second, entry_state, entry_second), jnp.where(second, exit_first, exit_adjoint)], -1
    )
    back = lax.ppermute(other, axis, [(i, i ^ 1) for i in range(count)])
    both = jnp.where(second, jnp.concatenate([back, mine], 0), jnp.concatenate([mine, back], 0))
    return both[..., :width], both[..., width:]


def head_ring(part, count, axis):
    return [part] + [
        lax.ppermute(part, axis, [(i, (i + k) % count) for i in range(count)])
        for k in range(1, count)
    ]


def make_body(seq_count, head_devices):
    def body(queries, raw_keys, values, write_rate, out_weight, out_grad):
        head_count = write_rate.shape[1]
        head_width = queries.shape[1] // head_count
        token_count = queries.shape[0]
        width = queries.shape[1]
        here = lax.axis_index("head")

        weight_rows = jnp.concatenate(
            [
                lax.dynamic_slice_in_dim(
                    out_weight, ((here - k) % head_devices) * width, width, 1
                )
                for k in range(head_devices)
            ],
            1,
        )

        def factor_inputs(float_query, float_key, float_value, rates):
            return block_factors(
                to_blocks(float_query, head_count),
                to_blocks(float_key, head_count),
                to_blocks(float_value, head_count),
                rate_blocks(rates),
            )

        factors, pull_factors = jax.vjp(
            factor_inputs,
            queries.astype(jnp.float32),
            raw_keys.astype(jnp.float32),
            values.astype(jnp.float32),
            write_rate,
        )
        unit_query, unit_key, key_mix, value_mix, causal_scores = factors
        late_grad, _ = lax.optimization_barrier((out_grad, key_mix))
        grad_parts = head_ring(late_grad, head_devices, "head")
        identity_heads = jnp.broadcast_to(
            jnp.eye(head_width, dtype=jnp.float32), (head_count, head_width, head_width)
        )
        zero_heads = jnp.zeros((head_count, head_width, head_width), jnp.float32)
        widened = (
            unit_query,
            unit_key,
            key_mix,
            jnp.concatenate([jnp.zeros_like(value_mix), value_mix], -1),
            causal_scores,
        )
        joined_state, joined_outputs = run_blocks(
            widened, jnp.concatenate([identity_heads, zero_heads], -1)
        )
        transition = joined_state[..., :head_width]
        offset = joined_state[..., head_width:]
        query_effect = joined_outputs[..., :head_width]
        attended_grad = lax.dot_general(
            jnp.concatenate(grad_parts, 1),
            weight_rows,
            (((1,), (1,)), ((), ())),
            preferred_element_type=jnp.float32,
        )
        grad_blocks = attended_grad.reshape(token_count // BLOCK, BLOCK, head_count, head_width)
        local_adjoint = jnp.einsum("nchd,nche->hde", query_effect, grad_blocks, precision=highest)
        weight_cols = [lax.dynamic_slice_in_dim(out_weight, here * width, width, 1)]
        for k in range(1, head_devices):
            block = lax.dynamic_slice_in_dim(
                out_weight, ((here + k) % head_devices) * width, width, 1
            )
            weight_cols.append(
                lax.ppermute(
                    block, "head", [(i, (i + k) % head_devices) for i in range(head_devices)]
                )
            )
        weight_mine = jnp.concatenate(weight_cols, 0)
        entry_state, exit_adjoint = scan_both(transition, offset, local_adjoint, seq_count, "seq")

        def run_from_entry(factor_tuple):
            return run_blocks(factor_tuple, entry_state)

        (final_state, block_outputs), pull_run = jax.vjp(run_from_entry, factors)
        attended_bf = from_blocks(block_outputs).astype(jnp.bfloat16)
        attended_parts = head_ring(attended_bf, head_devices, "head")
        layer_out = jnp.dot(
            jnp.concatenate(attended_parts, 1), weight_mine, preferred_element_type=jnp.float32
        ).astype(jnp.bfloat16)
        factor_grads = pull_run((exit_adjoint, grad_blocks))
        query_part, key_part, value_part, rate_grad = pull_factors(factor_grads[0])
        return (
            layer_out,
            query_part.astype(jnp.bfloat16),
            key_part.astype(jnp.bfloat16),
            value_part.astype(jnp.bfloat16),
            rate_grad,
        )

    return body


def solution(mesh):
    placed = (
        P("seq", "head"),
        P("seq", "head"),
        P("seq", "head"),
        P("seq", "head"),
        P("head", None),
        P("seq", "head"),
    )
    return jax.shard_map(
        make_body(mesh.shape["seq"], mesh.shape["head"]),
        mesh=mesh,
        in_specs=placed,
        out_specs=(
            P("seq", "head"),
            P("seq", "head"),
            P("seq", "head"),
            P("seq", "head"),
            P("seq", "head"),
        ),
        check_vma=False,
    )
```
